32 devices in a mesh: rep: 8 (over z, x), tile: 4 (over y, core).
Axes of the slice: x: 2, y: 2, z: 4, core: 2. Of those that a mesh axis runs over, the one named last changes fastest.
Arguments:
- features: bfloat16 [16, 48, 72, 1536], P('rep', 'tile'), may hold values from -6 to 6
- conv_out: bfloat16 [16, 48, 72, 256], P('rep', 'tile'), may hold values from -6 to 6
- conv_weight: bfloat16 [9, 1536, 256], replicated, may hold values from -0.0546875 to 0.0546875
- norm_gain_vector: float32 [256], replicated, may hold values from 0.5 to 1.5
- norm_shift_vector: float32 [256], replicated, may hold values from -3 to 3
- class_map: float32 [3, 256], replicated, may hold values from -3 to 3
- labels: int32 [16, 48, 72], P('rep', 'tile'), may hold values from 0 to 2
- class_weight: int32 [3], replicated, may hold values from 1 to 39
Outputs:
- grad_features: bfloat16 [16, 48, 72, 1536], P('rep', 'tile')
- grad_weight: float32 [1536, 9, 256], P(('rep', 'tile'))
- grad_gain: float32 [256], replicated
- grad_shift: float32 [256], replicated
- grad_class: float32 [3, 256], replicated
- loss: float32 [], replicated
The draws below stay inside these ranges and needn't reach their ends.
All inputs are finite; a program needn't handle non-finite values.
Results may differ from the reference program's by a relative error of at most 0.0049.
Values may be sent and summed in bfloat16 or wider, within the bound.
No kernel may reach another device: no remote copies, remote signals or barrier semaphores. Data moves between devices by JAX's collectives and lax.ppermute only.
A program may use at most 256 MiB of HBM per device.

```python
import jax
import jax.numpy as jnp
from jax import lax

IMG_DEV = 2
H = 48
W = 72
C_IN = 1536
C = 256
RATE = 12
CLASSES = 3
NB = 16
N_REP = 8


def draw_class_map(key, part):
    third_key = jax.random.fold_in(jax.random.fold_in(key, 17), 2)
    result = jnp.clip(0.25 * jax.random.normal(third_key, (CLASSES, C), jnp.float32), -3.0, 3.0)
    return result


def place_ends(entries, stream_key, smallest, high):
    spot = [jax.random.randint(jax.random.fold_in(stream_key, axis), (), 0, length) for axis, length in enumerate(entries.shape)]
    longest = entries.shape.index(max(entries.shape))
    neighbour = spot[:longest] + [(spot[longest] + 1) % entries.shape[longest]] + spot[longest + 1:]
    return entries.at[tuple(spot)].set(smallest).at[tuple(neighbour)].set(high)


def spiked(values, stream_key, source, target, blocks, factor):
    def block_of(axis_at):
        return (jnp.arange(values.shape[axis_at]) // (values.shape[axis_at] // blocks)).reshape((-1,) + (1,) * (values.ndim - 1 - axis_at))

    near = jax.random.permutation(stream_key, blocks)[block_of(target)]
    other_side = (block_of(target) + blocks // 2) % blocks
    return jnp.where((block_of(source) == near) | (block_of(source) == other_side), factor * values, values)


def block_levels(rng, dims, cuts, low, largest):
    def one(axis_at, shards_of):
        heights = jax.random.uniform(jax.random.fold_in(jax.random.fold_in(rng, 6), axis_at), (shards_of,), jnp.float32, low / len(cuts), largest / len(cuts))
        return jnp.repeat(jnp.exp(heights), dims[axis_at] // shards_of).reshape((-1,) + (1,) * (len(dims) - axis_at - 1))

    factor_of = one(*cuts[0])
    for cut in cuts[1:]:
        factor_of = factor_of * one(*cut)
    return factor_of


def scatter_about(stream_key, shape, width, reach, cuts=(), kind=jnp.bfloat16):
    values = width * jax.random.normal(stream_key, shape, jnp.float32)
    if cuts:
        values = values * block_levels(stream_key, shape, cuts, -0.22, 0.18)
    return jnp.clip(values, -reach, reach).astype(kind)


def bell_draw_with(own_key, shape, spread, bound, shards, heavy, held_as=jnp.bfloat16):
    values = spread * jax.random.normal(own_key, shape, jnp.float32)
    if shards:
        values = values * block_levels(own_key, shape, shards, -0.22, 0.18)
    return jnp.clip(spiked(values, jax.random.fold_in(own_key, 3), *heavy), -bound, bound).astype(held_as)


def setup_inputs(seed: int = 0) -> dict:
    key_list = jax.random.split(jax.random.key(seed), 9)
    return {
        "features": bell_draw_with(key_list[0], (NB, H, W, C_IN), 1.0, 6.0, ((0, 8), (1, 4)), (0, 3, 8, 2.0)),
        "conv_out": scatter_about(key_list[1], (NB, H, W, C), 1.0, 6.0, ((0, 8), (1, 4))),
        "conv_weight": scatter_about(key_list[2], (9, C_IN, C), (9 * C_IN) ** -0.5, 0.0546875),
        "norm_gain_vector": jnp.clip(1.0 + 0.1 * jax.random.normal(key_list[3], (C,), jnp.float32), 0.5, 1.5),
        "norm_shift_vector": scatter_about(key_list[4], (C,), 0.5, 3.0, (), jnp.float32),
        "class_map": draw_class_map(jax.random.fold_in(key_list[8], 71), 0),
        "labels": place_ends(jax.random.randint(key_list[6], (NB, H, W), 0, 3), jax.random.fold_in(key_list[6], 1), 0, 2).astype(jnp.int32),
        "class_weight": jax.random.randint(key_list[7], (CLASSES,), 1, 40).astype(jnp.int32),
    }


def reference(features, conv_out, conv_weight, norm_gain_vector, norm_shift_vector, class_map, labels, class_weight):
    highest = lax.Precision.HIGHEST
    pixels = H * W
    per_replica_part = IMG_DEV * pixels
    yvals = conv_out.astype(jnp.float32).reshape(N_REP, per_replica_part, C)
    centre_offset = yvals - lax.optimization_barrier(jnp.sum(yvals, 1, keepdims=True)) / per_replica_part
    variance = lax.optimization_barrier(jnp.sum(centre_offset * centre_offset, 1, keepdims=True)) / per_replica_part
    inverse_deviation = lax.rsqrt(variance + 1e-05)
    normalized_input = centre_offset * inverse_deviation
    preactivation_values = norm_gain_vector * normalized_input + norm_shift_vector
    zvals = jnp.maximum(preactivation_values, 0.0)
    logits = jnp.einsum('rpc,qc->rpq', zvals, class_map, precision=highest)
    label_flat = labels.reshape(N_REP, per_replica_part)
    onehot = (label_flat[..., None] == jnp.arange(CLASSES, dtype=jnp.int32)).astype(jnp.float32)
    weights_pix = lax.optimization_barrier(jnp.sum(onehot * class_weight.astype(jnp.float32), -1))
    top_val = lax.optimization_barrier(jnp.max(logits, -1, keepdims=True))
    log_total = top_val[..., 0] + jnp.log(lax.optimization_barrier(jnp.sum(jnp.exp(logits - top_val), -1)))
    cross = log_total - lax.optimization_barrier(jnp.sum(onehot * logits, -1))
    all_pix = NB * pixels
    mean_weight = jnp.sum(weights_pix) / all_pix
    loss = jnp.sum(weights_pix * cross) / mean_weight / all_pix
    probs = jnp.exp(logits - log_total[..., None])
    grad_logit = (weights_pix / mean_weight)[..., None] * (probs - onehot)
    grad_class = jnp.einsum('rpq,rpc->qc', grad_logit, zvals, precision=highest)
    grad_z = jnp.einsum('rpq,qc->rpc', grad_logit, class_map, precision=highest)
    preactivation_gradient = jnp.where(preactivation_values > 0, grad_z, 0.0)
    first_gradient_sum = lax.optimization_barrier(jnp.sum(preactivation_gradient, 1, keepdims=True))
    second_gradient_sum = lax.optimization_barrier(jnp.sum(preactivation_gradient * normalized_input, 1, keepdims=True))
    grad_shift = lax.optimization_barrier(jnp.sum(first_gradient_sum, (0, 1)))
    grad_gain = lax.optimization_barrier(jnp.sum(second_gradient_sum, (0, 1)))
    normalized_output_gradient = (norm_gain_vector * inverse_deviation * (preactivation_gradient - first_gradient_sum / per_replica_part - normalized_input * second_gradient_sum / per_replica_part)).astype(jnp.bfloat16)
    normalized_output_gradient = normalized_output_gradient.reshape(NB, H, W, C)

    def one_image(carry, inputs):
        image, grad_img = inputs
        padded = jnp.pad(grad_img, ((RATE, RATE), (RATE, RATE), (0, 0)))
        flat_x = image.reshape(pixels, C_IN)
        accum = jnp.zeros((pixels, C_IN), jnp.float32)
        pieces = []
        for tap_index in range(9):
            row_off = RATE - (tap_index // 3 - 1) * RATE
            col_off = RATE - (tap_index % 3 - 1) * RATE
            shifted = padded[row_off:row_off + H, col_off:col_off + W].reshape(pixels, C)
            accum = accum + lax.dot_general(shifted, conv_weight[tap_index], (((1,), (1,)), ((), ())), preferred_element_type=jnp.float32)
            pieces.append(lax.dot_general(flat_x, shifted, (((0,), (0,)), ((), ())), preferred_element_type=jnp.float32))
        return (carry + jnp.stack(pieces, 1), accum.astype(jnp.bfloat16).reshape(H, W, C_IN))
    grad_weight, grad_features = lax.scan(one_image, jnp.zeros((C_IN, 9, C), jnp.float32), (features, normalized_output_gradient))
    return (grad_features, grad_weight, grad_gain, grad_shift, grad_class, loss)
```

```python
import jax
import jax.numpy as jnp
from jax import lax
from jax.sharding import PartitionSpec as P

IMG_DEV = 2
H = 48
W = 72
RATE = 12


def padded(x, sides, width):
    for axis, dim in sides:
        size, length = (lax.axis_size(axis), x.shape[dim])
        up = [(i, (i + 1) % size) for i in range(size - 1)]
        down = [(j, i) for i, j in up]
        last = lax.slice_in_dim(x, length - width, length, axis=dim)
        first = lax.slice_in_dim(x, 0, width, axis=dim)
        before = lax.ppermute(last, axis, up)
        after = lax.ppermute(first, axis, down)
        x = jnp.concatenate([before, x, after], axis=dim)
    return x


def index_bits(axes):
    bits = []
    for axis in reversed(axes):
        size = lax.axis_size(axis)
        assert size & (size - 1) == 0
        bits += [(axis, b) for b in range(size.bit_length() - 1)]
    return bits


def exchange(x, axis, bit):
    size = lax.axis_size(axis)
    pairs = [(i, i ^ (1 << bit)) for i in range(size)]
    return lax.ppermute(x, axis, pairs)


def butterfly_sum(x, axes):
    for axis, bit in index_bits(axes):
        x = jax.tree.map(lambda v, w: v + w, x, exchange(x, axis, bit))
    return x


def halving_scatter(x, axes):
    for axis, bit in index_bits(axes):
        mine = (lax.axis_index(axis) >> bit) & 1
        x = x.reshape((2, x.shape[0] // 2) + x.shape[1:])
        keep = lax.dynamic_index_in_dim(x, mine, 0, keepdims=False)
        send = lax.dynamic_index_in_dim(x, 1 - mine, 0, keepdims=False)
        x = keep + exchange(send, axis, bit)
    return x


def body(
    features,
    conv_out,
    conv_weight,
    norm_gain_vector,
    norm_shift_vector,
    class_map,
    labels,
    class_weight,
):
    highest = lax.Precision.HIGHEST
    images, tile_rows, columns, in_chans = features.shape
    out_chans = conv_out.shape[3]
    taps = conv_weight.shape[0]
    local_pix = images * tile_rows * columns
    per_replica_part = IMG_DEV * H * W
    all_pix = lax.axis_size("rep") * per_replica_part
    classes = class_map.shape[0]

    onehot = (
        labels.reshape(local_pix, 1) == jnp.arange(classes, dtype=jnp.int32)
    ).astype(jnp.float32)
    weights_pix = jnp.sum(onehot * class_weight.astype(jnp.float32), -1)
    weight_total = butterfly_sum(jnp.sum(weights_pix), ("rep", "tile"))

    yvals = conv_out.astype(jnp.float32).reshape(local_pix, out_chans)
    column_sum = lax.psum(jnp.sum(yvals, 0), "tile")
    centre_offset = yvals - column_sum / per_replica_part
    variance = lax.psum(jnp.sum(centre_offset * centre_offset, 0), "tile") / per_replica_part
    inverse_deviation = lax.rsqrt(variance + 1e-05)
    normalized_input = centre_offset * inverse_deviation
    preactivation_values = norm_gain_vector * normalized_input + norm_shift_vector
    zvals = jnp.maximum(preactivation_values, 0.0)
    logits = jnp.dot(zvals, class_map.T, precision=highest)
    top_val = jnp.max(logits, -1, keepdims=True)
    log_total = top_val[:, 0] + jnp.log(jnp.sum(jnp.exp(logits - top_val), -1))
    cross = log_total - jnp.sum(onehot * logits, -1)
    mean_weight = weight_total / all_pix
    probs = jnp.exp(logits - log_total[:, None])
    grad_logit = (weights_pix / mean_weight)[:, None] * (probs - onehot)
    class_local_slice = jnp.dot(grad_logit.T, zvals, precision=highest)
    grad_z = jnp.dot(grad_logit, class_map, precision=highest)
    preactivation_gradient = jnp.where(preactivation_values > 0, grad_z, 0.0)
    first_gradient_sum, second_gradient_sum, class_tile, loss_tile = lax.psum(
        (
            jnp.sum(preactivation_gradient, 0),
            jnp.sum(preactivation_gradient * normalized_input, 0),
            class_local_slice,
            jnp.sum(weights_pix * cross),
        ),
        "tile",
    )
    grad_shift, grad_gain, grad_class, loss_total = butterfly_sum(
        (first_gradient_sum, second_gradient_sum, class_tile, loss_tile), ("rep",)
    )
    loss = loss_total / mean_weight / all_pix
    normalized_output_gradient = (
        norm_gain_vector
        * inverse_deviation
        * (
            preactivation_gradient
            - first_gradient_sum / per_replica_part
            - normalized_input * second_gradient_sum / per_replica_part
        )
    ).astype(jnp.bfloat16)
    normalized_output_gradient = normalized_output_gradient.reshape(
        images, tile_rows, columns, out_chans
    )
    extended = padded(normalized_output_gradient, (("tile", 1),), RATE)
    extended = jnp.pad(extended, ((0, 0), (0, 0), (RATE, RATE), (0, 0)))
    shifted_list = []
    for tap_index in range(taps):
        row_off = RATE - (tap_index // 3 - 1) * RATE
        col_off = RATE - (tap_index % 3 - 1) * RATE
        piece = extended[:, row_off : row_off + tile_rows, col_off : col_off + columns, :]
        shifted_list.append(piece.reshape(local_pix, 1, out_chans))
    shifted = jnp.concatenate(shifted_list, 1)

    blocks = lax.axis_size("rep") * lax.axis_size("tile")
    nbits = blocks.bit_length() - 1
    flat_x = features.reshape((local_pix,) + (2,) * nbits + (in_chans // blocks,))
    flat_x = flat_x.transpose((0,) + tuple(range(nbits, 0, -1)) + (nbits + 1,))
    flat_x = flat_x.reshape(local_pix, in_chans)
    weight_part = lax.dot_general(
        flat_x, shifted, (((0,), (0,)), ((), ())), preferred_element_type=jnp.float32
    )
    grad_weight = halving_scatter(weight_part, ("rep", "tile"))

    accum_grad = lax.dot_general(
        shifted,
        conv_weight,
        (((1, 2), (0, 2)), ((), ())),
        preferred_element_type=jnp.float32,
    )
    grad_features = accum_grad.astype(jnp.bfloat16).reshape(images, tile_rows, columns, in_chans)
    return (grad_features, grad_weight, grad_gain, grad_shift, grad_class, loss)


def solution(mesh):
    in_specs = (
        P("rep", "tile", None, None),
        P("rep", "tile", None, None),
        P(),
        P(),
        P(),
        P(),
        P("rep", "tile", None),
        P(),
    )
    out_specs = (P("rep", "tile", None, None), P(("rep", "tile"), None, None), P(), P(), P(), P())
    return jax.shard_map(body, mesh=mesh, in_specs=in_specs, out_specs=out_specs, check_vma=False)
```

```python
import jax
import jax.numpy as jnp
from jax import lax
from jax.sharding import PartitionSpec as P

IMG_DEV = 2
H = 48
W = 72
RATE = 12


def padded(x, sides, width):
    for axis, dim in sides:
        size, length = (lax.axis_size(axis), x.shape[dim])
        up = [(i, (i + 1) % size) for i in range(size - 1)]
        down = [(j, i) for i, j in up]
        last = lax.slice_in_dim(x, length - width, length, axis=dim)
        first = lax.slice_in_dim(x, 0, width, axis=dim)
        before = lax.ppermute(last, axis, up)
        after = lax.ppermute(first, axis, down)
        x = jnp.concatenate([before, x, after], axis=dim)
    return x


def index_bits(axes):
    bits = []
    for axis in reversed(axes):
        size = lax.axis_size(axis)
        assert size & (size - 1) == 0
        bits += [(axis, b) for b in range(size.bit_length() - 1)]
    return bits


def exchange(x, axis, bit):
    size = lax.axis_size(axis)
    pairs = [(i, i ^ (1 << bit)) for i in range(size)]
    return lax.ppermute(x, axis, pairs)


def butterfly_sum(x, axes):
    for axis, bit in index_bits(axes):
        x = jax.tree.map(lambda v, w: v + w, x, exchange(x, axis, bit))
    return x


def halving_scatter(x, steps, bit_axes):
    bit_axes = list(bit_axes)
    for axis, bit, combined in steps:
        ax = bit_axes.index(combined)
        mine = (lax.axis_index(axis) >> bit) & 1
        keep = lax.dynamic_index_in_dim(x, mine, ax, keepdims=False)
        send = lax.dynamic_index_in_dim(x, 1 - mine, ax, keepdims=False)
        x = keep + exchange(send, axis, bit)
        bit_axes.pop(ax)
    return x


def body(
    features,
    conv_out,
    conv_weight,
    norm_gain_vector,
    norm_shift_vector,
    class_map,
    labels,
    class_weight,
):
    highest = lax.Precision.HIGHEST
    images, tile_rows, columns, in_chans = features.shape
    out_chans = conv_out.shape[3]
    taps = conv_weight.shape[0]
    local_pix = images * tile_rows * columns
    per_replica_part = IMG_DEV * H * W
    all_pix = lax.axis_size("rep") * per_replica_part
    classes = class_map.shape[0]

    onehot = (
        labels.reshape(local_pix, 1) == jnp.arange(classes, dtype=jnp.int32)
    ).astype(jnp.float32)
    weights_pix = jnp.sum(onehot * class_weight.astype(jnp.float32), -1)

    yvals = conv_out.astype(jnp.float32).reshape(local_pix, out_chans)
    column_sum, weight_tile = lax.psum((jnp.sum(yvals, 0), jnp.sum(weights_pix)), "tile")
    weight_total = butterfly_sum(weight_tile, ("rep",))
    centre_offset = yvals - column_sum / per_replica_part
    variance = lax.psum(jnp.sum(centre_offset * centre_offset, 0), "tile") / per_replica_part
    inverse_deviation = lax.rsqrt(variance + 1e-05)
    normalized_input = centre_offset * inverse_deviation
    preactivation_values = norm_gain_vector * normalized_input + norm_shift_vector
    zvals = jnp.maximum(preactivation_values, 0.0)
    logits = jnp.dot(zvals, class_map.T, precision=highest)
    top_val = jnp.max(logits, -1, keepdims=True)
    log_total = top_val[:, 0] + jnp.log(jnp.sum(jnp.exp(logits - top_val), -1))
    cross = log_total - jnp.sum(onehot * logits, -1)
    mean_weight = weight_total / all_pix
    probs = jnp.exp(logits - log_total[:, None])
    grad_logit = (weights_pix / mean_weight)[:, None] * (probs - onehot)
    class_local_slice = jnp.dot(grad_logit.T, zvals, precision=highest)
    grad_z = jnp.dot(grad_logit, class_map, precision=highest)
    preactivation_gradient = jnp.where(preactivation_values > 0, grad_z, 0.0)
    first_gradient_sum, second_gradient_sum, class_tile, loss_tile = lax.psum(
        (
            jnp.sum(preactivation_gradient, 0),
            jnp.sum(preactivation_gradient * normalized_input, 0),
            class_local_slice,
            jnp.sum(weights_pix * cross),
        ),
        "tile",
    )
    grad_shift, grad_gain, grad_class, loss_total = butterfly_sum(
        (first_gradient_sum, second_gradient_sum, class_tile, loss_tile), ("rep",)
    )
    loss = loss_total / mean_weight / all_pix
    normalized_output_gradient = (
        norm_gain_vector
        * inverse_deviation
        * (
            preactivation_gradient
            - first_gradient_sum / per_replica_part
            - normalized_input * second_gradient_sum / per_replica_part
        )
    ).astype(jnp.bfloat16)
    normalized_output_gradient = normalized_output_gradient.reshape(
        images, tile_rows, columns, out_chans
    )
    extended = padded(normalized_output_gradient, (("tile", 1),), RATE)
    extended = jnp.pad(extended, ((0, 0), (0, 0), (RATE, RATE), (0, 0)))
    shifted_list = []
    for tap_index in range(taps):
        row_off = RATE - (tap_index // 3 - 1) * RATE
        col_off = RATE - (tap_index % 3 - 1) * RATE
        piece = extended[:, row_off : row_off + tile_rows, col_off : col_off + columns, :]
        shifted_list.append(piece.reshape(local_pix, 1, out_chans))
    shifted = jnp.concatenate(shifted_list, 1)

    blocks = lax.axis_size("rep") * lax.axis_size("tile")
    nbits = blocks.bit_length() - 1
    flat_x = features.reshape(local_pix, in_chans)
    weight_part = lax.dot_general(
        flat_x, shifted, (((0,), (0,)), ((), ())), preferred_element_type=jnp.float32
    )
    weight_part = weight_part.reshape((2,) * nbits + (in_chans // blocks, taps, out_chans))
    bits = [(axis, bit, combined) for combined, (axis, bit) in enumerate(index_bits(("rep", "tile")))]
    bit_axes = list(range(nbits - 1, -1, -1))

    accum_grad = lax.dot_general(
        shifted,
        conv_weight,
        (((1, 2), (0, 2)), ((), ())),
        preferred_element_type=jnp.float32,
    )
    axis, bit, combined = bits[0]
    ax = bit_axes.index(combined)
    mine = (lax.axis_index(axis) >> bit) & 1
    keep = lax.dynamic_index_in_dim(weight_part, mine, ax, keepdims=False)
    send = lax.dynamic_index_in_dim(weight_part, 1 - mine, ax, keepdims=False)
    received, accum_grad = lax.optimization_barrier((exchange(send, axis, bit), accum_grad))
    half = keep + received
    bit_axes.pop(ax)
    rest = bits[1:]
    streams = 3
    per = taps // streams
    pieces = []
    for s in range(streams):
        order = rest[s:] + rest[:s]
        chunk = lax.slice_in_dim(half, s * per, (s + 1) * per if s < streams - 1 else taps, axis=half.ndim - 2)
        pieces.append(halving_scatter(chunk, order, bit_axes))
    grad_weight = jnp.concatenate(pieces, 1)

    grad_features = accum_grad.astype(jnp.bfloat16).reshape(images, tile_rows, columns, in_chans)
    return (grad_features, grad_weight, grad_gain, grad_shift, grad_class, loss)


def solution(mesh):
    in_specs = (
        P("rep", "tile", None, None),
        P("rep", "tile", None, None),
        P(),
        P(),
        P(),
        P(),
        P("rep", "tile", None),
        P(),
    )
    out_specs = (P("rep", "tile", None, None), P(("rep", "tile"), None, None), P(), P(), P(), P())
    return jax.shard_map(body, mesh=mesh, in_specs=in_specs, out_specs=out_specs, check_vma=False)
```

```python
import jax
import jax.numpy as jnp
from jax import lax
from jax.sharding import PartitionSpec as P

IMG_DEV = 2
H = 48
W = 72
RATE = 12


def padded(x, sides, width):
    for axis, dim in sides:
        size, length = (lax.axis_size(axis), x.shape[dim])
        up = [(i, (i + 1) % size) for i in range(size - 1)]
        down = [(j, i) for i, j in up]
        last = lax.slice_in_dim(x, length - width, length, axis=dim)
        first = lax.slice_in_dim(x, 0, width, axis=dim)
        before = lax.ppermute(last, axis, up)
        after = lax.ppermute(first, axis, down)
        x = jnp.concatenate([before, x, after], axis=dim)
    return x


def index_bits(axes):
    bits = []
    for axis in reversed(axes):
        size = lax.axis_size(axis)
        assert size & (size - 1) == 0
        bits += [(axis, b) for b in range(size.bit_length() - 1)]
    return bits


def exchange(x, axis, bit):
    size = lax.axis_size(axis)
    pairs = [(i, i ^ (1 << bit)) for i in range(size)]
    return lax.ppermute(x, axis, pairs)


def butterfly_sum(x, axes):
    for axis, bit in index_bits(axes):
        x = jax.tree.map(lambda v, w: v + w, x, exchange(x, axis, bit))
    return x


def halving_scatter(x, steps, bit_axes):
    bit_axes = list(bit_axes)
    for axis, bit, combined in steps:
        ax = bit_axes.index(combined)
        mine = (lax.axis_index(axis) >> bit) & 1
        keep = lax.dynamic_index_in_dim(x, mine, ax, keepdims=False)
        send = lax.dynamic_index_in_dim(x, 1 - mine, ax, keepdims=False)
        x = keep + exchange(send, axis, bit)
        bit_axes.pop(ax)
    return x


def body(
    features,
    conv_out,
    conv_weight,
    norm_gain_vector,
    norm_shift_vector,
    class_map,
    labels,
    class_weight,
):
    highest = lax.Precision.HIGHEST
    images, tile_rows, columns, in_chans = features.shape
    out_chans = conv_out.shape[3]
    taps = conv_weight.shape[0]
    local_pix = images * tile_rows * columns
    per_replica_part = IMG_DEV * H * W
    all_pix = lax.axis_size("rep") * per_replica_part
    classes = class_map.shape[0]

    onehot = (
        labels.reshape(local_pix, 1) == jnp.arange(classes, dtype=jnp.int32)
    ).astype(jnp.float32)
    weights_pix = jnp.sum(onehot * class_weight.astype(jnp.float32), -1)

    yvals = conv_out.astype(jnp.float32).reshape(local_pix, out_chans)
    first_sums = lax.psum(jnp.concatenate([jnp.sum(yvals, 0), jnp.sum(weights_pix)[None]]), "tile")
    column_sum, weight_tile = first_sums[:out_chans], first_sums[out_chans]
    weight_total = butterfly_sum(weight_tile, ("rep",))
    centre_offset = yvals - column_sum / per_replica_part
    variance = lax.psum(jnp.sum(centre_offset * centre_offset, 0), "tile") / per_replica_part
    inverse_deviation = lax.rsqrt(variance + 1e-05)
    normalized_input = centre_offset * inverse_deviation
    preactivation_values = norm_gain_vector * normalized_input + norm_shift_vector
    zvals = jnp.maximum(preactivation_values, 0.0)
    logits = jnp.dot(zvals, class_map.T, precision=highest)
    top_val = jnp.max(logits, -1, keepdims=True)
    log_total = top_val[:, 0] + jnp.log(jnp.sum(jnp.exp(logits - top_val), -1))
    cross = log_total - jnp.sum(onehot * logits, -1)
    mean_weight = weight_total / all_pix
    probs = jnp.exp(logits - log_total[:, None])
    grad_logit = (weights_pix / mean_weight)[:, None] * (probs - onehot)
    class_local_slice = jnp.dot(grad_logit.T, zvals, precision=highest)
    grad_z = jnp.dot(grad_logit, class_map, precision=highest)
    preactivation_gradient = jnp.where(preactivation_values > 0, grad_z, 0.0)
    first_gradient_sum, second_gradient_sum, class_tile, loss_tile = lax.psum(
        (
            jnp.sum(preactivation_gradient, 0),
            jnp.sum(preactivation_gradient * normalized_input, 0),
            class_local_slice,
            jnp.sum(weights_pix * cross),
        ),
        "tile",
    )
    grad_shift, grad_gain, grad_class, loss_total = butterfly_sum(
        (first_gradient_sum, second_gradient_sum, class_tile, loss_tile), ("rep",)
    )
    loss = loss_total / mean_weight / all_pix
    normalized_output_gradient = (
        norm_gain_vector
        * inverse_deviation
        * (
            preactivation_gradient
            - first_gradient_sum / per_replica_part
            - normalized_input * second_gradient_sum / per_replica_part
        )
    ).astype(jnp.bfloat16)
    normalized_output_gradient = normalized_output_gradient.reshape(
        images, tile_rows, columns, out_chans
    )
    extended = padded(normalized_output_gradient, (("tile", 1),), RATE)
    extended = jnp.pad(extended, ((0, 0), (0, 0), (RATE, RATE), (0, 0)))
    shifted_list = []
    for tap_index in range(taps):
        row_off = RATE - (tap_index // 3 - 1) * RATE
        col_off = RATE - (tap_index % 3 - 1) * RATE
        piece = extended[:, row_off : row_off + tile_rows, col_off : col_off + columns, :]
        shifted_list.append(piece.reshape(local_pix, out_chans))
    shifted = jnp.concatenate(shifted_list, 1)

    blocks = lax.axis_size("rep") * lax.axis_size("tile")
    nbits = blocks.bit_length() - 1
    rows = in_chans // blocks
    flat_x = features.reshape(local_pix, in_chans)
    bits = [(axis, bit, combined) for combined, (axis, bit) in enumerate(index_bits(("rep", "tile")))]
    streams = 3
    per = taps // streams
    parts = []
    for s in range(streams):
        cols = shifted[:, s * per * out_chans : (s + 1) * per * out_chans]
        part = lax.dot_general(
            flat_x, cols, (((0,), (0,)), ((), ())), preferred_element_type=jnp.float32
        )
        parts.append(part.reshape((2,) * nbits + (rows, per * out_chans)))

    accum_grad = lax.dot_general(
        shifted.reshape(local_pix, taps, out_chans),
        conv_weight,
        (((1, 2), (0, 2)), ((), ())),
        preferred_element_type=jnp.float32,
    )
    axis, bit, combined = bits[0]
    bit_axes = list(range(nbits - 1, -1, -1))
    ax = bit_axes.index(combined)
    mine = (lax.axis_index(axis) >> bit) & 1
    keeps = [lax.dynamic_index_in_dim(p, mine, ax, keepdims=False) for p in parts]
    sends = [lax.dynamic_index_in_dim(p, 1 - mine, ax, keepdims=False) for p in parts]
    received, accum_grad = lax.optimization_barrier(
        ([exchange(v, axis, bit) for v in sends], accum_grad)
    )
    bit_axes.pop(ax)
    rest = bits[1:]
    pieces = []
    for s in range(streams):
        order = rest[s:] + rest[:s]
        pieces.append(halving_scatter(keeps[s] + received[s], order, bit_axes))
    grad_weight = jnp.concatenate(pieces, 1).reshape(rows, taps, out_chans)

    grad_features = accum_grad.astype(jnp.bfloat16).reshape(images, tile_rows, columns, in_chans)
    return (grad_features, grad_weight, grad_gain, grad_shift, grad_class, loss)


def solution(mesh):
    in_specs = (
        P("rep", "tile", None, None),
        P("rep", "tile", None, None),
        P(),
        P(),
        P(),
        P(),
        P("rep", "tile", None),
        P(),
    )
    out_specs = (P("rep", "tile", None, None), P(("rep", "tile"), None, None), P(), P(), P(), P())
    return jax.shard_map(body, mesh=mesh, in_specs=in_specs, out_specs=out_specs, check_vma=False)
```

```python
import jax
import jax.numpy as jnp
from jax import lax
from jax.sharding import PartitionSpec as P

IMG_DEV = 2
H = 48
W = 72
RATE = 12


def padded(x, sides, width):
    for axis, dim in sides:
        size, length = (lax.axis_size(axis), x.shape[dim])
        up = [(i, (i + 1) % size) for i in range(size - 1)]
        down = [(j, i) for i, j in up]
        last = lax.slice_in_dim(x, length - width, length, axis=dim)
        first = lax.slice_in_dim(x, 0, width, axis=dim)
        before = lax.ppermute(last, axis, up)
        after = lax.ppermute(first, axis, down)
        x = jnp.concatenate([before, x, after], axis=dim)
    return x


def index_bits(axes):
    bits = []
    for axis in reversed(axes):
        size = lax.axis_size(axis)
        assert size & (size - 1) == 0
        bits += [(axis, b) for b in range(size.bit_length() - 1)]
    return bits


def exchange(x, axis, bit):
    size = lax.axis_size(axis)
    pairs = [(i, i ^ (1 << bit)) for i in range(size)]
    return lax.ppermute(x, axis, pairs)


def butterfly_sum(x, axes):
    for axis, bit in index_bits(axes):
        x = jax.tree.map(lambda v, w: v + w, x, exchange(x, axis, bit))
    return x


def halving_scatter(x, steps, bit_axes):
    bit_axes = list(bit_axes)
    for axis, bit, combined in steps:
        ax = bit_axes.index(combined)
        mine = (lax.axis_index(axis) >> bit) & 1
        keep = lax.dynamic_index_in_dim(x, mine, ax, keepdims=False)
        send = lax.dynamic_index_in_dim(x, 1 - mine, ax, keepdims=False)
        x = keep + exchange(send, axis, bit)
        bit_axes.pop(ax)
    return x


def body(
    features,
    conv_out,
    conv_weight,
    norm_gain_vector,
    norm_shift_vector,
    class_map,
    labels,
    class_weight,
):
    highest = lax.Precision.HIGHEST
    images, tile_rows, columns, in_chans = features.shape
    out_chans = conv_out.shape[3]
    taps = conv_weight.shape[0]
    local_pix = images * tile_rows * columns
    per_replica_part = IMG_DEV * H * W
    all_pix = lax.axis_size("rep") * per_replica_part
    classes = class_map.shape[0]

    onehot = (
        labels.reshape(local_pix, 1) == jnp.arange(classes, dtype=jnp.int32)
    ).astype(jnp.float32)
    weights_pix = jnp.sum(onehot * class_weight.astype(jnp.float32), -1)

    yvals = conv_out.astype(jnp.float32).reshape(local_pix, out_chans)
    first_sums = lax.psum(jnp.concatenate([jnp.sum(yvals, 0), jnp.sum(weights_pix)[None]]), "tile")
    column_sum, weight_tile = first_sums[:out_chans], first_sums[out_chans]
    weight_total = butterfly_sum(weight_tile, ("rep",))
    centre_offset = yvals - column_sum / per_replica_part
    variance = lax.psum(jnp.sum(centre_offset * centre_offset, 0), "tile") / per_replica_part
    inverse_deviation = lax.rsqrt(variance + 1e-05)
    normalized_input = centre_offset * inverse_deviation
    preactivation_values = norm_gain_vector * normalized_input + norm_shift_vector
    zvals = jnp.maximum(preactivation_values, 0.0)
    logits = jnp.dot(zvals, class_map.T, precision=highest)
    top_val = jnp.max(logits, -1, keepdims=True)
    log_total = top_val[:, 0] + jnp.log(jnp.sum(jnp.exp(logits - top_val), -1))
    cross = log_total - jnp.sum(onehot * logits, -1)
    mean_weight = weight_total / all_pix
    probs = jnp.exp(logits - log_total[:, None])
    grad_logit = (weights_pix / mean_weight)[:, None] * (probs - onehot)
    class_local_slice = jnp.dot(grad_logit.T, zvals, precision=highest)
    grad_z = jnp.dot(grad_logit, class_map, precision=highest)
    preactivation_gradient = jnp.where(preactivation_values > 0, grad_z, 0.0)
    first_gradient_sum, second_gradient_sum, class_tile, loss_tile = lax.psum(
        (
            jnp.sum(preactivation_gradient, 0),
            jnp.sum(preactivation_gradient * normalized_input, 0),
            class_local_slice,
            jnp.sum(weights_pix * cross),
        ),
        "tile",
    )
    packed = jnp.concatenate(
        [first_gradient_sum, second_gradient_sum, class_tile.reshape(-1), loss_tile[None]]
    )
    packed = butterfly_sum(packed, ("rep",))
    normalized_output_gradient = (
        norm_gain_vector
        * inverse_deviation
        * (
            preactivation_gradient
            - first_gradient_sum / per_replica_part
            - normalized_input * second_gradient_sum / per_replica_part
        )
    ).astype(jnp.bfloat16)
    normalized_output_gradient = normalized_output_gradient.reshape(
        images, tile_rows, columns, out_chans
    )
    extended = padded(normalized_output_gradient, (("tile", 1),), RATE)
    extended = jnp.pad(extended, ((0, 0), (0, 0), (RATE, RATE), (0, 0)))
    shifted_list = []
    for tap_index in range(taps):
        row_off = RATE - (tap_index // 3 - 1) * RATE
        col_off = RATE - (tap_index % 3 - 1) * RATE
        piece = extended[:, row_off : row_off + tile_rows, col_off : col_off + columns, :]
        shifted_list.append(piece.reshape(local_pix, out_chans))
    shifted = jnp.concatenate(shifted_list, 1)
    packed, shifted = lax.optimization_barrier((packed, shifted))
    grad_shift = packed[:out_chans]
    grad_gain = packed[out_chans : 2 * out_chans]
    grad_class = packed[2 * out_chans : (2 + classes) * out_chans].reshape(classes, out_chans)
    loss = packed[(2 + classes) * out_chans] / mean_weight / all_pix

    blocks = lax.axis_size("rep") * lax.axis_size("tile")
    nbits = blocks.bit_length() - 1
    rows = in_chans // blocks
    flat_x = features.reshape(local_pix, in_chans)
    bits = [(axis, bit, combined) for combined, (axis, bit) in enumerate(index_bits(("rep", "tile")))]
    rest = bits[1:]
    orders = [rest, rest[1:2] + rest[:1] + rest[2:], rest[2:] + rest[:2]]
    group_taps = [taps - 2 * (taps // 3) + 1, taps // 3, taps // 3 - 1]
    starts = [sum(group_taps[:s]) for s in range(3)]
    parts = []
    for s in range(3):
        cols = shifted[:, starts[s] * out_chans : (starts[s] + group_taps[s]) * out_chans]
        part = lax.dot_general(
            flat_x, cols, (((0,), (0,)), ((), ())), preferred_element_type=jnp.float32
        )
        parts.append(part.reshape((2,) * nbits + (rows, group_taps[s] * out_chans)))

    accum_grad = lax.dot_general(
        shifted.reshape(local_pix, taps, out_chans),
        conv_weight,
        (((1, 2), (0, 2)), ((), ())),
        preferred_element_type=jnp.float32,
    )
    axis, bit, combined = bits[0]
    bit_axes = list(range(nbits - 1, -1, -1))
    ax = bit_axes.index(combined)
    mine = (lax.axis_index(axis) >> bit) & 1
    keeps = [lax.dynamic_index_in_dim(p, mine, ax, keepdims=False) for p in parts]
    sends = [lax.dynamic_index_in_dim(p, 1 - mine, ax, keepdims=False) for p in parts]
    received, accum_grad = lax.optimization_barrier(
        ([exchange(v, axis, bit) for v in sends], accum_grad)
    )
    bit_axes.pop(ax)
    pieces = []
    for s in range(3):
        pieces.append(halving_scatter(keeps[s] + received[s], orders[s], bit_axes))
    grad_weight = jnp.concatenate(pieces, 1).reshape(rows, taps, out_chans)

    grad_features = accum_grad.astype(jnp.bfloat16).reshape(images, tile_rows, columns, in_chans)
    return (grad_features, grad_weight, grad_gain, grad_shift, grad_class, loss)


def solution(mesh):
    in_specs = (
        P("rep", "tile", None, None),
        P("rep", "tile", None, None),
        P(),
        P(),
        P(),
        P(),
        P("rep", "tile", None),
        P(),
    )
    out_specs = (P("rep", "tile", None, None), P(("rep", "tile"), None, None), P(), P(), P(), P())
    return jax.shard_map(body, mesh=mesh, in_specs=in_specs, out_specs=out_specs, check_vma=False)
```

```python
import jax
import jax.numpy as jnp
from jax import lax
from jax.sharding import PartitionSpec as P

IMG_DEV = 2
H = 48
W = 72
RATE = 12


def padded(x, sides, width):
    for axis, dim in sides:
        size, length = (lax.axis_size(axis), x.shape[dim])
        up = [(i, (i + 1) % size) for i in range(size - 1)]
        down = [(j, i) for i, j in up]
        last = lax.slice_in_dim(x, length - width, length, axis=dim)
        first = lax.slice_in_dim(x, 0, width, axis=dim)
        before = lax.ppermute(last, axis, up)
        after = lax.ppermute(first, axis, down)
        x = jnp.concatenate([before, x, after], axis=dim)
    return x


def index_bits(axes):
    bits = []
    for axis in reversed(axes):
        size = lax.axis_size(axis)
        assert size & (size - 1) == 0
        bits += [(axis, b) for b in range(size.bit_length() - 1)]
    return bits


def exchange(x, axis, bit):
    size = lax.axis_size(axis)
    pairs = [(i, i ^ (1 << bit)) for i in range(size)]
    return lax.ppermute(x, axis, pairs)


def butterfly_sum(x, axes):
    for axis, bit in index_bits(axes):
        x = jax.tree.map(lambda v, w: v + w, x, exchange(x, axis, bit))
    return x


def halving_scatter(x, steps, bit_axes):
    bit_axes = list(bit_axes)
    for axis, bit, combined in steps:
        ax = bit_axes.index(combined)
        mine = (lax.axis_index(axis) >> bit) & 1
        keep = lax.dynamic_index_in_dim(x, mine, ax, keepdims=False)
        send = lax.dynamic_index_in_dim(x, 1 - mine, ax, keepdims=False)
        x = keep + exchange(send, axis, bit)
        bit_axes.pop(ax)
    return x


def body(
    features,
    conv_out,
    conv_weight,
    norm_gain_vector,
    norm_shift_vector,
    class_map,
    labels,
    class_weight,
):
    highest = lax.Precision.HIGHEST
    images, tile_rows, columns, in_chans = features.shape
    out_chans = conv_out.shape[3]
    taps = conv_weight.shape[0]
    local_pix = images * tile_rows * columns
    per_replica_part = IMG_DEV * H * W
    all_pix = lax.axis_size("rep") * per_replica_part
    classes = class_map.shape[0]

    onehot = (
        labels.reshape(local_pix, 1) == jnp.arange(classes, dtype=jnp.int32)
    ).astype(jnp.float32)
    weights_pix = jnp.sum(onehot * class_weight.astype(jnp.float32), -1)

    yvals = conv_out.astype(jnp.float32).reshape(local_pix, out_chans)
    first_sums = lax.psum(jnp.concatenate([jnp.sum(yvals, 0), jnp.sum(weights_pix)[None]]), "tile")
    column_sum, weight_tile = first_sums[:out_chans], first_sums[out_chans]
    weight_total = butterfly_sum(weight_tile, ("rep",))
    centre_offset = yvals - column_sum / per_replica_part
    variance = lax.psum(jnp.sum(centre_offset * centre_offset, 0), "tile") / per_replica_part
    inverse_deviation = lax.rsqrt(variance + 1e-05)
    normalized_input = centre_offset * inverse_deviation
    preactivation_values = norm_gain_vector * normalized_input + norm_shift_vector
    zvals = jnp.maximum(preactivation_values, 0.0)
    logits = jnp.dot(zvals, class_map.T, precision=highest)
    top_val = jnp.max(logits, -1, keepdims=True)
    log_total = top_val[:, 0] + jnp.log(jnp.sum(jnp.exp(logits - top_val), -1))
    cross = log_total - jnp.sum(onehot * logits, -1)
    mean_weight = weight_total / all_pix
    probs = jnp.exp(logits - log_total[:, None])
    grad_logit = (weights_pix / mean_weight)[:, None] * (probs - onehot)
    class_local_slice = jnp.dot(grad_logit.T, zvals, precision=highest)
    grad_z = jnp.dot(grad_logit, class_map, precision=highest)
    preactivation_gradient = jnp.where(preactivation_values > 0, grad_z, 0.0)
    first_gradient_sum, second_gradient_sum, class_tile, loss_tile = lax.psum(
        (
            jnp.sum(preactivation_gradient, 0),
            jnp.sum(preactivation_gradient * normalized_input, 0),
            class_local_slice,
            jnp.sum(weights_pix * cross),
        ),
        "tile",
    )
    packed = jnp.concatenate(
        [first_gradient_sum, second_gradient_sum, class_tile.reshape(-1), loss_tile[None]]
    )
    packed = butterfly_sum(packed, ("rep",))
    normalized_output_gradient = (
        norm_gain_vector
        * inverse_deviation
        * (
            preactivation_gradient
            - first_gradient_sum / per_replica_part
            - normalized_input * second_gradient_sum / per_replica_part
        )
    ).astype(jnp.bfloat16)
    normalized_output_gradient = normalized_output_gradient.reshape(
        images, tile_rows, columns, out_chans
    )
    extended = padded(normalized_output_gradient, (("tile", 1),), RATE)
    extended = jnp.pad(extended, ((0, 0), (0, 0), (RATE, RATE), (0, 0)))
    shifted_list = []
    for tap_index in range(taps):
        row_off = RATE - (tap_index // 3 - 1) * RATE
        col_off = RATE - (tap_index % 3 - 1) * RATE
        piece = extended[:, row_off : row_off + tile_rows, col_off : col_off + columns, :]
        shifted_list.append(piece.reshape(local_pix, out_chans))
    shifted = jnp.concatenate(shifted_list, 1)
    grad_shift = packed[:out_chans]
    grad_gain = packed[out_chans : 2 * out_chans]
    grad_class = packed[2 * out_chans : (2 + classes) * out_chans].reshape(classes, out_chans)
    loss = packed[(2 + classes) * out_chans] / mean_weight / all_pix

    blocks = lax.axis_size("rep") * lax.axis_size("tile")
    nbits = blocks.bit_length() - 1
    rows = in_chans // blocks
    flat_x = features.reshape(local_pix, in_chans)
    packed, flat_x = lax.optimization_barrier((packed, flat_x))
    bits = [(axis, bit, combined) for combined, (axis, bit) in enumerate(index_bits(("rep", "tile")))]
    rest = bits[1:]
    orders = [rest[s:] + rest[:s] for s in range(3)]
    group_taps = [taps - 2 * (taps // 3), taps // 3, taps // 3]
    starts = [sum(group_taps[:s]) for s in range(3)]
    parts = []
    for s in range(3):
        cols = shifted[:, starts[s] * out_chans : (starts[s] + group_taps[s]) * out_chans]
        part = lax.dot_general(
            flat_x, cols, (((0,), (0,)), ((), ())), preferred_element_type=jnp.float32
        )
        parts.append(part.reshape((2,) * nbits + (rows, group_taps[s] * out_chans)))

    accum_grad = lax.dot_general(
        shifted.reshape(local_pix, taps, out_chans),
        conv_weight,
        (((1, 2), (0, 2)), ((), ())),
        preferred_element_type=jnp.float32,
    )
    axis, bit, combined = bits[0]
    bit_axes = list(range(nbits - 1, -1, -1))
    ax = bit_axes.index(combined)
    mine = (lax.axis_index(axis) >> bit) & 1
    keeps = [lax.dynamic_index_in_dim(p, mine, ax, keepdims=False) for p in parts]
    sends = [lax.dynamic_index_in_dim(p, 1 - mine, ax, keepdims=False) for p in parts]
    received, accum_grad = lax.optimization_barrier(
        ([exchange(v, axis, bit) for v in sends], accum_grad)
    )
    bit_axes.pop(ax)
    pieces = [keeps[s] + received[s] for s in range(3)]
    axes_of = [list(bit_axes) for s in range(3)]
    for step in range(len(rest)):
        sends, keeps = [], []
        for s in range(3):
            axis, bit, combined = orders[s][step]
            ax = axes_of[s].index(combined)
            mine = (lax.axis_index(axis) >> bit) & 1
            keeps.append(lax.dynamic_index_in_dim(pieces[s], mine, ax, keepdims=False))
            sends.append(lax.dynamic_index_in_dim(pieces[s], 1 - mine, ax, keepdims=False))
            axes_of[s].pop(ax)
        received = lax.optimization_barrier(
            [exchange(sends[s], orders[s][step][0], orders[s][step][1]) for s in range(3)]
        )
        pieces = [keeps[s] + received[s] for s in range(3)]
    grad_weight = jnp.concatenate(pieces, 1).reshape(rows, taps, out_chans)

    grad_features = accum_grad.astype(jnp.bfloat16).reshape(images, tile_rows, columns, in_chans)
    return (grad_features, grad_weight, grad_gain, grad_shift, grad_class, loss)


def solution(mesh):
    in_specs = (
        P("rep", "tile", None, None),
        P("rep", "tile", None, None),
        P(),
        P(),
        P(),
        P(),
        P("rep", "tile", None),
        P(),
    )
    out_specs = (P("rep", "tile", None, None), P(("rep", "tile"), None, None), P(), P(), P(), P())
    return jax.shard_map(body, mesh=mesh, in_specs=in_specs, out_specs=out_specs, check_vma=False)
```

```python
import jax
import jax.numpy as jnp
from jax import lax
from jax.sharding import PartitionSpec as P

IMG_DEV = 2
H = 48
W = 72
RATE = 12


def padded(x, sides, width):
    for axis, dim in sides:
        size, length = (lax.axis_size(axis), x.shape[dim])
        up = [(i, (i + 1) % size) for i in range(size - 1)]
        down = [(j, i) for i, j in up]
        last = lax.slice_in_dim(x, length - width, length, axis=dim)
        first = lax.slice_in_dim(x, 0, width, axis=dim)
        before = lax.ppermute(last, axis, up)
        after = lax.ppermute(first, axis, down)
        x = jnp.concatenate([before, x, after], axis=dim)
    return x


def index_bits(axes):
    bits = []
    for axis in reversed(axes):
        size = lax.axis_size(axis)
        assert size & (size - 1) == 0
        bits += [(axis, b) for b in range(size.bit_length() - 1)]
    return bits


def exchange(x, axis, bit):
    size = lax.axis_size(axis)
    pairs = [(i, i ^ (1 << bit)) for i in range(size)]
    return lax.ppermute(x, axis, pairs)


def butterfly_sum(x, axes):
    for axis, bit in index_bits(axes):
        x = jax.tree.map(lambda v, w: v + w, x, exchange(x, axis, bit))
    return x


def halving_scatter(x, steps, bit_axes):
    bit_axes = list(bit_axes)
    for axis, bit, combined in steps:
        ax = bit_axes.index(combined)
        mine = (lax.axis_index(axis) >> bit) & 1
        keep = lax.dynamic_index_in_dim(x, mine, ax, keepdims=False)
        send = lax.dynamic_index_in_dim(x, 1 - mine, ax, keepdims=False)
        x = keep + exchange(send, axis, bit)
        bit_axes.pop(ax)
    return x


def body(
    features,
    conv_out,
    conv_weight,
    norm_gain_vector,
    norm_shift_vector,
    class_map,
    labels,
    class_weight,
):
    highest = lax.Precision.HIGHEST
    images, tile_rows, columns, in_chans = features.shape
    out_chans = conv_out.shape[3]
    taps = conv_weight.shape[0]
    local_pix = images * tile_rows * columns
    per_replica_part = IMG_DEV * H * W
    all_pix = lax.axis_size("rep") * per_replica_part
    classes = class_map.shape[0]

    onehot = (
        labels.reshape(local_pix, 1) == jnp.arange(classes, dtype=jnp.int32)
    ).astype(jnp.float32)
    weights_pix = jnp.sum(onehot * class_weight.astype(jnp.float32), -1)

    yvals = conv_out.astype(jnp.float32).reshape(local_pix, out_chans)
    first_sums = lax.psum(jnp.concatenate([jnp.sum(yvals, 0), jnp.sum(weights_pix)[None]]), "tile")
    column_sum, weight_tile = first_sums[:out_chans], first_sums[out_chans]
    weight_total = butterfly_sum(weight_tile, ("rep",))
    centre_offset = yvals - column_sum / per_replica_part
    variance = lax.psum(jnp.sum(centre_offset * centre_offset, 0), "tile") / per_replica_part
    inverse_deviation = lax.rsqrt(variance + 1e-05)
    normalized_input = centre_offset * inverse_deviation
    preactivation_values = norm_gain_vector * normalized_input + norm_shift_vector
    zvals = jnp.maximum(preactivation_values, 0.0)
    logits = jnp.dot(zvals, class_map.T, precision=highest)
    top_val = jnp.max(logits, -1, keepdims=True)
    log_total = top_val[:, 0] + jnp.log(jnp.sum(jnp.exp(logits - top_val), -1))
    cross = log_total - jnp.sum(onehot * logits, -1)
    mean_weight = weight_total / all_pix
    probs = jnp.exp(logits - log_total[:, None])
    grad_logit = (weights_pix / mean_weight)[:, None] * (probs - onehot)
    class_local_slice = jnp.dot(grad_logit.T, zvals, precision=highest)
    grad_z = jnp.dot(grad_logit, class_map, precision=highest)
    preactivation_gradient = jnp.where(preactivation_values > 0, grad_z, 0.0)
    first_gradient_sum, second_gradient_sum, class_tile, loss_tile = lax.psum(
        (
            jnp.sum(preactivation_gradient, 0),
            jnp.sum(preactivation_gradient * normalized_input, 0),
            class_local_slice,
            jnp.sum(weights_pix * cross),
        ),
        "tile",
    )
    packed = jnp.concatenate(
        [first_gradient_sum, second_gradient_sum, class_tile.reshape(-1), loss_tile[None]]
    )
    packed = butterfly_sum(packed, ("rep",))
    normalized_output_gradient = (
        norm_gain_vector
        * inverse_deviation
        * (
            preactivation_gradient
            - first_gradient_sum / per_replica_part
            - normalized_input * second_gradient_sum / per_replica_part
        )
    ).astype(jnp.bfloat16)
    normalized_output_gradient = normalized_output_gradient.reshape(
        images, tile_rows, columns, out_chans
    )
    extended = padded(normalized_output_gradient, (("tile", 1),), RATE)
    extended = jnp.pad(extended, ((0, 0), (0, 0), (RATE, RATE), (0, 0)))
    shifted_list = []
    for tap_index in range(taps):
        row_off = RATE - (tap_index // 3 - 1) * RATE
        col_off = RATE - (tap_index % 3 - 1) * RATE
        piece = extended[:, row_off : row_off + tile_rows, col_off : col_off + columns, :]
        shifted_list.append(piece.reshape(local_pix, out_chans))
    shifted = jnp.concatenate(shifted_list, 1)
    grad_shift = packed[:out_chans]
    grad_gain = packed[out_chans : 2 * out_chans]
    grad_class = packed[2 * out_chans : (2 + classes) * out_chans].reshape(classes, out_chans)
    loss = packed[(2 + classes) * out_chans] / mean_weight / all_pix

    blocks = lax.axis_size("rep") * lax.axis_size("tile")
    nbits = blocks.bit_length() - 1
    rows = in_chans // blocks
    flat_x = features.reshape(local_pix, in_chans)
    packed, flat_x = lax.optimization_barrier((packed, flat_x))
    bits = [(axis, bit, combined) for combined, (axis, bit) in enumerate(index_bits(("rep", "tile")))]
    rest = bits[1:]
    orders = [rest, rest[1:] + rest[:1], rest[2:3] + rest[:2] + rest[3:]]
    group_taps = [taps - 2 * (taps // 3), taps // 3, taps // 3]
    starts = [sum(group_taps[:s]) for s in range(3)]
    parts = []
    for s in range(3):
        cols = shifted[:, starts[s] * out_chans : (starts[s] + group_taps[s]) * out_chans]
        part = lax.dot_general(
            flat_x, cols, (((0,), (0,)), ((), ())), preferred_element_type=jnp.float32
        )
        parts.append(part.reshape((2,) * nbits + (rows, group_taps[s] * out_chans)))

    halves = 2 if images % 2 == 0 else 1
    share = local_pix // halves
    grad_chunks = [
        lax.dot_general(
            shifted[h * share : (h + 1) * share].reshape(share, taps, out_chans),
            conv_weight,
            (((1, 2), (0, 2)), ((), ())),
            preferred_element_type=jnp.float32,
        ).astype(jnp.bfloat16)
        for h in range(halves)
    ]
    axis, bit, combined = bits[0]
    bit_axes = list(range(nbits - 1, -1, -1))
    ax = bit_axes.index(combined)
    mine = (lax.axis_index(axis) >> bit) & 1
    keeps = [lax.dynamic_index_in_dim(p, mine, ax, keepdims=False) for p in parts]
    sends = [lax.dynamic_index_in_dim(p, 1 - mine, ax, keepdims=False) for p in parts]
    received = lax.optimization_barrier([exchange(v, axis, bit) for v in sends])
    bit_axes.pop(ax)
    pieces = [keeps[s] + received[s] for s in range(3)]
    axes_of = [list(bit_axes) for s in range(3)]
    for step in range(len(rest)):
        sends, keeps = [], []
        for s in range(3):
            axis, bit, combined = orders[s][step]
            ax = axes_of[s].index(combined)
            mine = (lax.axis_index(axis) >> bit) & 1
            keeps.append(lax.dynamic_index_in_dim(pieces[s], mine, ax, keepdims=False))
            sends.append(lax.dynamic_index_in_dim(pieces[s], 1 - mine, ax, keepdims=False))
            axes_of[s].pop(ax)
        received = [exchange(sends[s], orders[s][step][0], orders[s][step][1]) for s in range(3)]
        if step < halves:
            received, grad_chunks[step] = lax.optimization_barrier((received, grad_chunks[step]))
        else:
            received = lax.optimization_barrier(received)
        pieces = [keeps[s] + received[s] for s in range(3)]
    grad_weight = jnp.concatenate(pieces, 1).reshape(rows, taps, out_chans)

    grad_features = jnp.concatenate(grad_chunks, 0).reshape(images, tile_rows, columns, in_chans)
    return (grad_features, grad_weight, grad_gain, grad_shift, grad_class, loss)


def solution(mesh):
    in_specs = (
        P("rep", "tile", None, None),
        P("rep", "tile", None, None),
        P(),
        P(),
        P(),
        P(),
        P("rep", "tile", None),
        P(),
    )
    out_specs = (P("rep", "tile", None, None), P(("rep", "tile"), None, None), P(), P(), P(), P())
    return jax.shard_map(body, mesh=mesh, in_specs=in_specs, out_specs=out_specs, check_vma=False)
```

```python
import jax
import jax.numpy as jnp
from jax import lax
from jax.sharding import PartitionSpec as P

IMG_DEV = 2
H = 48
W = 72
RATE = 12


def padded(x, sides, width):
    for axis, dim in sides:
        size, length = (lax.axis_size(axis), x.shape[dim])
        up = [(i, (i + 1) % size) for i in range(size - 1)]
        down = [(j, i) for i, j in up]
        last = lax.slice_in_dim(x, length - width, length, axis=dim)
        first = lax.slice_in_dim(x, 0, width, axis=dim)
        before = lax.ppermute(last, axis, up)
        after = lax.ppermute(first, axis, down)
        x = jnp.concatenate([before, x, after], axis=dim)
    return x


def index_bits(axes):
    bits = []
    for axis in reversed(axes):
        size = lax.axis_size(axis)
        assert size & (size - 1) == 0
        bits += [(axis, b) for b in range(size.bit_length() - 1)]
    return bits


def exchange(x, axis, bit):
    size = lax.axis_size(axis)
    pairs = [(i, i ^ (1 << bit)) for i in range(size)]
    return lax.ppermute(x, axis, pairs)


def butterfly_sum(x, axes):
    for axis, bit in index_bits(axes):
        x = jax.tree.map(lambda v, w: v + w, x, exchange(x, axis, bit))
    return x


def halving_scatter(x, steps, bit_axes):
    bit_axes = list(bit_axes)
    for axis, bit, combined in steps:
        ax = bit_axes.index(combined)
        mine = (lax.axis_index(axis) >> bit) & 1
        keep = lax.dynamic_index_in_dim(x, mine, ax, keepdims=False)
        send = lax.dynamic_index_in_dim(x, 1 - mine, ax, keepdims=False)
        x = keep + exchange(send, axis, bit)
        bit_axes.pop(ax)
    return x


def body(
    features,
    conv_out,
    conv_weight,
    norm_gain_vector,
    norm_shift_vector,
    class_map,
    labels,
    class_weight,
):
    highest = lax.Precision.HIGHEST
    images, tile_rows, columns, in_chans = features.shape
    out_chans = conv_out.shape[3]
    taps = conv_weight.shape[0]
    local_pix = images * tile_rows * columns
    per_replica_part = IMG_DEV * H * W
    all_pix = lax.axis_size("rep") * per_replica_part
    classes = class_map.shape[0]

    onehot = (
        labels.reshape(local_pix, 1) == jnp.arange(classes, dtype=jnp.int32)
    ).astype(jnp.float32)
    weights_pix = jnp.sum(onehot * class_weight.astype(jnp.float32), -1)

    yvals = conv_out.astype(jnp.float32).reshape(local_pix, out_chans)
    first_sums = lax.psum(jnp.concatenate([jnp.sum(yvals, 0), jnp.sum(weights_pix)[None]]), "tile")
    column_sum, weight_tile = first_sums[:out_chans], first_sums[out_chans]
    weight_total = butterfly_sum(weight_tile, ("rep",))
    centre_offset = yvals - column_sum / per_replica_part
    variance = lax.psum(jnp.sum(centre_offset * centre_offset, 0), "tile") / per_replica_part
    inverse_deviation = lax.rsqrt(variance + 1e-05)
    normalized_input = centre_offset * inverse_deviation
    preactivation_values = norm_gain_vector * normalized_input + norm_shift_vector
    zvals = jnp.maximum(preactivation_values, 0.0)
    logits = jnp.dot(zvals, class_map.T, precision=highest)
    top_val = jnp.max(logits, -1, keepdims=True)
    log_total = top_val[:, 0] + jnp.log(jnp.sum(jnp.exp(logits - top_val), -1))
    cross = log_total - jnp.sum(onehot * logits, -1)
    mean_weight = weight_total / all_pix
    probs = jnp.exp(logits - log_total[:, None])
    grad_logit = (weights_pix / mean_weight)[:, None] * (probs - onehot)
    class_local_slice = jnp.dot(grad_logit.T, zvals, precision=highest)
    grad_z = jnp.dot(grad_logit, class_map, precision=highest)
    preactivation_gradient = jnp.where(preactivation_values > 0, grad_z, 0.0)
    first_gradient_sum, second_gradient_sum, class_tile, loss_tile = lax.psum(
        (
            jnp.sum(preactivation_gradient, 0),
            jnp.sum(preactivation_gradient * normalized_input, 0),
            class_local_slice,
            jnp.sum(weights_pix * cross),
        ),
        "tile",
    )
    packed = jnp.concatenate(
        [first_gradient_sum, second_gradient_sum, class_tile.reshape(-1), loss_tile[None]]
    )
    normalized_output_gradient = (
        norm_gain_vector
        * inverse_deviation
        * (
            preactivation_gradient
            - first_gradient_sum / per_replica_part
            - normalized_input * second_gradient_sum / per_replica_part
        )
    ).astype(jnp.bfloat16)
    normalized_output_gradient = normalized_output_gradient.reshape(
        images, tile_rows, columns, out_chans
    )
    extended = padded(normalized_output_gradient, (("tile", 1),), RATE)
    extended = jnp.pad(extended, ((0, 0), (0, 0), (RATE, RATE), (0, 0)))
    shifted_list = []
    for tap_index in range(taps):
        row_off = RATE - (tap_index // 3 - 1) * RATE
        col_off = RATE - (tap_index % 3 - 1) * RATE
        piece = extended[:, row_off : row_off + tile_rows, col_off : col_off + columns, :]
        shifted_list.append(piece.reshape(local_pix, out_chans))
    shifted = jnp.concatenate(shifted_list, 1)

    blocks = lax.axis_size("rep") * lax.axis_size("tile")
    nbits = blocks.bit_length() - 1
    rows = in_chans // blocks
    flat_x = features.reshape(local_pix, in_chans)
    bits = [(axis, bit, combined) for combined, (axis, bit) in enumerate(index_bits(("rep", "tile")))]
    rest = bits[1:]
    orders = [rest, rest[1:] + rest[:1], rest[2:3] + rest[:2] + rest[3:]]
    group_taps = [taps - 2 * (taps // 3), taps // 3, taps // 3]
    starts = [sum(group_taps[:s]) for s in range(3)]
    parts = []
    for s in range(3):
        cols = shifted[:, starts[s] * out_chans : (starts[s] + group_taps[s]) * out_chans]
        part = lax.dot_general(
            flat_x, cols, (((0,), (0,)), ((), ())), preferred_element_type=jnp.float32
        )
        parts.append(part.reshape((2,) * nbits + (rows, group_taps[s] * out_chans)))

    halves = 2
    share = in_chans // halves
    grad_chunks = [
        lax.dot_general(
            shifted.reshape(local_pix, taps, out_chans),
            conv_weight[:, h * share : (h + 1) * share, :],
            (((1, 2), (0, 2)), ((), ())),
            preferred_element_type=jnp.float32,
        ).astype(jnp.bfloat16)
        for h in range(halves)
    ]
    axis, bit, combined = bits[0]
    bit_axes = list(range(nbits - 1, -1, -1))
    ax = bit_axes.index(combined)
    mine = (lax.axis_index(axis) >> bit) & 1
    keeps = [lax.dynamic_index_in_dim(p, mine, ax, keepdims=False) for p in parts]
    sends = [lax.dynamic_index_in_dim(p, 1 - mine, ax, keepdims=False) for p in parts]
    received = lax.optimization_barrier([exchange(v, axis, bit) for v in sends])
    bit_axes.pop(ax)
    pieces = [keeps[s] + received[s] for s in range(3)]
    small_bits = index_bits(("rep",))
    axes_of = [list(bit_axes) for s in range(3)]
    for step in range(len(rest)):
        sends, keeps = [], []
        for s in range(3):
            axis, bit, combined = orders[s][step]
            ax = axes_of[s].index(combined)
            mine = (lax.axis_index(axis) >> bit) & 1
            keeps.append(lax.dynamic_index_in_dim(pieces[s], mine, ax, keepdims=False))
            sends.append(lax.dynamic_index_in_dim(pieces[s], 1 - mine, ax, keepdims=False))
            axes_of[s].pop(ax)
        received = [exchange(sends[s], orders[s][step][0], orders[s][step][1]) for s in range(3)]
        if step < len(small_bits):
            received.append(exchange(packed, *small_bits[step]))
        if step < halves:
            received, grad_chunks[step] = lax.optimization_barrier((received, grad_chunks[step]))
        else:
            received = lax.optimization_barrier(received)
        if step < len(small_bits):
            packed = packed + received.pop()
        pieces = [keeps[s] + received[s] for s in range(3)]
    grad_weight = jnp.concatenate(pieces, 1).reshape(rows, taps, out_chans)

    for step in range(len(rest), len(small_bits)):
        packed = packed + exchange(packed, *small_bits[step])
    grad_shift = packed[:out_chans]
    grad_gain = packed[out_chans : 2 * out_chans]
    grad_class = packed[2 * out_chans : (2 + classes) * out_chans].reshape(classes, out_chans)
    loss = packed[(2 + classes) * out_chans] / mean_weight / all_pix
    grad_features = jnp.concatenate(grad_chunks, 1).reshape(images, tile_rows, columns, in_chans)
    return (grad_features, grad_weight, grad_gain, grad_shift, grad_class, loss)


def solution(mesh):
    in_specs = (
        P("rep", "tile", None, None),
        P("rep", "tile", None, None),
        P(),
        P(),
        P(),
        P(),
        P("rep", "tile", None),
        P(),
    )
    out_specs = (P("rep", "tile", None, None), P(("rep", "tile"), None, None), P(), P(), P(), P())
    return jax.shard_map(body, mesh=mesh, in_specs=in_specs, out_specs=out_specs, check_vma=False)
```

```python
import jax
import jax.numpy as jnp
from jax import lax
from jax.sharding import PartitionSpec as P

IMG_DEV = 2
H = 48
W = 72
RATE = 12


def padded(x, sides, width):
    for axis, dim in sides:
        size, length = (lax.axis_size(axis), x.shape[dim])
        up = [(i, (i + 1) % size) for i in range(size - 1)]
        down = [(j, i) for i, j in up]
        last = lax.slice_in_dim(x, length - width, length, axis=dim)
        first = lax.slice_in_dim(x, 0, width, axis=dim)
        before = lax.ppermute(last, axis, up)
        after = lax.ppermute(first, axis, down)
        x = jnp.concatenate([before, x, after], axis=dim)
    return x


def index_bits(axes):
    bits = []
    for axis in reversed(axes):
        size = lax.axis_size(axis)
        assert size & (size - 1) == 0
        bits += [(axis, b) for b in range(size.bit_length() - 1)]
    return bits


def exchange(x, axis, bit):
    size = lax.axis_size(axis)
    pairs = [(i, i ^ (1 << bit)) for i in range(size)]
    return lax.ppermute(x, axis, pairs)


def butterfly_sum(x, axes):
    for axis, bit in index_bits(axes):
        x = jax.tree.map(lambda v, w: v + w, x, exchange(x, axis, bit))
    return x


def halving_scatter(x, steps, bit_axes):
    bit_axes = list(bit_axes)
    for axis, bit, combined in steps:
        ax = bit_axes.index(combined)
        mine = (lax.axis_index(axis) >> bit) & 1
        keep = lax.dynamic_index_in_dim(x, mine, ax, keepdims=False)
        send = lax.dynamic_index_in_dim(x, 1 - mine, ax, keepdims=False)
        x = keep + exchange(send, axis, bit)
        bit_axes.pop(ax)
    return x


def body(
    features,
    conv_out,
    conv_weight,
    norm_gain_vector,
    norm_shift_vector,
    class_map,
    labels,
    class_weight,
):
    highest = lax.Precision.HIGHEST
    images, tile_rows, columns, in_chans = features.shape
    out_chans = conv_out.shape[3]
    taps = conv_weight.shape[0]
    local_pix = images * tile_rows * columns
    per_replica_part = IMG_DEV * H * W
    all_pix = lax.axis_size("rep") * per_replica_part
    classes = class_map.shape[0]

    onehot = (
        labels.reshape(local_pix, 1) == jnp.arange(classes, dtype=jnp.int32)
    ).astype(jnp.float32)
    weights_pix = jnp.sum(onehot * class_weight.astype(jnp.float32), -1)

    yvals = conv_out.astype(jnp.float32).reshape(local_pix, out_chans)
    first_sums = lax.psum(jnp.concatenate([jnp.sum(yvals, 0), jnp.sum(weights_pix)[None]]), "tile")
    column_sum, weight_tile = first_sums[:out_chans], first_sums[out_chans]
    weight_total = butterfly_sum(weight_tile, ("rep",))
    centre_offset = yvals - column_sum / per_replica_part
    variance = lax.psum(jnp.sum(centre_offset * centre_offset, 0), "tile") / per_replica_part
    inverse_deviation = lax.rsqrt(variance + 1e-05)
    normalized_input = centre_offset * inverse_deviation
    preactivation_values = norm_gain_vector * normalized_input + norm_shift_vector
    zvals = jnp.maximum(preactivation_values, 0.0)
    logits = jnp.dot(zvals, class_map.T, precision=highest)
    top_val = jnp.max(logits, -1, keepdims=True)
    log_total = top_val[:, 0] + jnp.log(jnp.sum(jnp.exp(logits - top_val), -1))
    cross = log_total - jnp.sum(onehot * logits, -1)
    mean_weight = weight_total / all_pix
    probs = jnp.exp(logits - log_total[:, None])
    grad_logit = (weights_pix / mean_weight)[:, None] * (probs - onehot)
    class_local_slice = jnp.dot(grad_logit.T, zvals, precision=highest)
    grad_z = jnp.dot(grad_logit, class_map, precision=highest)
    preactivation_gradient = jnp.where(preactivation_values > 0, grad_z, 0.0)
    first_gradient_sum, second_gradient_sum, class_tile, loss_tile = lax.psum(
        (
            jnp.sum(preactivation_gradient, 0),
            jnp.sum(preactivation_gradient * normalized_input, 0),
            class_local_slice,
            jnp.sum(weights_pix * cross),
        ),
        "tile",
    )
    packed = jnp.concatenate(
        [first_gradient_sum, second_gradient_sum, class_tile.reshape(-1), loss_tile[None]]
    )
    normalized_output_gradient = (
        norm_gain_vector
        * inverse_deviation
        * (
            preactivation_gradient
            - first_gradient_sum / per_replica_part
            - normalized_input * second_gradient_sum / per_replica_part
        )
    ).astype(jnp.bfloat16)
    normalized_output_gradient = normalized_output_gradient.reshape(
        images, tile_rows, columns, out_chans
    )
    extended = padded(normalized_output_gradient, (("tile", 1),), RATE)
    extended = jnp.pad(extended, ((0, 0), (0, 0), (RATE, RATE), (0, 0)))
    shifted_list = []
    for tap_index in range(taps):
        row_off = RATE - (tap_index // 3 - 1) * RATE
        col_off = RATE - (tap_index % 3 - 1) * RATE
        piece = extended[:, row_off : row_off + tile_rows, col_off : col_off + columns, :]
        shifted_list.append(piece.reshape(local_pix, out_chans))
    shifted = jnp.concatenate(shifted_list, 1)

    blocks = lax.axis_size("rep") * lax.axis_size("tile")
    nbits = blocks.bit_length() - 1
    rows = in_chans // blocks
    flat_x = features.reshape(local_pix, in_chans)
    packed, flat_x = lax.optimization_barrier((packed, flat_x))
    bits = [(axis, bit, combined) for combined, (axis, bit) in enumerate(index_bits(("rep", "tile")))]
    rest = bits[1:]
    orders = [rest, rest[1:] + rest[:1], rest[2:3] + rest[:2] + rest[3:]]
    group_taps = [taps - 2 * (taps // 3), taps // 3, taps // 3]
    starts = [sum(group_taps[:s]) for s in range(3)]
    parts = []
    for s in range(3):
        cols = shifted[:, starts[s] * out_chans : (starts[s] + group_taps[s]) * out_chans]
        part = lax.dot_general(
            flat_x, cols, (((0,), (0,)), ((), ())), preferred_element_type=jnp.float32
        )
        parts.append(part.reshape((2,) * nbits + (rows, group_taps[s] * out_chans)))

    halves = 2 if images % 2 == 0 else 1
    share = local_pix // halves
    grad_chunks = [
        lax.dot_general(
            shifted[h * share : (h + 1) * share].reshape(share, taps, out_chans),
            conv_weight,
            (((1, 2), (0, 2)), ((), ())),
            preferred_element_type=jnp.float32,
        ).astype(jnp.bfloat16)
        for h in range(halves)
    ]
    axis, bit, combined = bits[0]
    bit_axes = list(range(nbits - 1, -1, -1))
    ax = bit_axes.index(combined)
    mine = (lax.axis_index(axis) >> bit) & 1
    keeps = [lax.dynamic_index_in_dim(p, mine, ax, keepdims=False) for p in parts]
    sends = [lax.dynamic_index_in_dim(p, 1 - mine, ax, keepdims=False) for p in parts]
    received = lax.optimization_barrier([exchange(v, axis, bit) for v in sends])
    bit_axes.pop(ax)
    pieces = [keeps[s] + received[s] for s in range(3)]
    small_bits = index_bits(("rep",))
    axes_of = [list(bit_axes) for s in range(3)]
    for step in range(len(rest)):
        sends, keeps = [], []
        for s in range(3):
            axis, bit, combined = orders[s][step]
            ax = axes_of[s].index(combined)
            mine = (lax.axis_index(axis) >> bit) & 1
            keeps.append(lax.dynamic_index_in_dim(pieces[s], mine, ax, keepdims=False))
            sends.append(lax.dynamic_index_in_dim(pieces[s], 1 - mine, ax, keepdims=False))
            axes_of[s].pop(ax)
        received = [exchange(sends[s], orders[s][step][0], orders[s][step][1]) for s in range(3)]
        if step < len(small_bits):
            received.append(exchange(packed, *small_bits[step]))
        if step < halves:
            received, grad_chunks[step] = lax.optimization_barrier((received, grad_chunks[step]))
        else:
            received = lax.optimization_barrier(received)
        if step < len(small_bits):
            packed = packed + received.pop()
        pieces = [keeps[s] + received[s] for s in range(3)]
    grad_weight = jnp.concatenate(pieces, 1).reshape(rows, taps, out_chans)

    for step in range(len(rest), len(small_bits)):
        packed = packed + exchange(packed, *small_bits[step])
    grad_shift = packed[:out_chans]
    grad_gain = packed[out_chans : 2 * out_chans]
    grad_class = packed[2 * out_chans : (2 + classes) * out_chans].reshape(classes, out_chans)
    loss = packed[(2 + classes) * out_chans] / mean_weight / all_pix
    grad_features = jnp.concatenate(grad_chunks, 0).reshape(images, tile_rows, columns, in_chans)
    return (grad_features, grad_weight, grad_gain, grad_shift, grad_class, loss)


def solution(mesh):
    in_specs = (
        P("rep", "tile", None, None),
        P("rep", "tile", None, None),
        P(),
        P(),
        P(),
        P(),
        P("rep", "tile", None),
        P(),
    )
    out_specs = (P("rep", "tile", None, None), P(("rep", "tile"), None, None), P(), P(), P(), P())
    return jax.shard_map(body, mesh=mesh, in_specs=in_specs, out_specs=out_specs, check_vma=False)
```

```python
import jax
import jax.numpy as jnp
from jax import lax
from jax.sharding import PartitionSpec as P

IMG_DEV = 2
H = 48
W = 72
RATE = 12


def padded(x, sides, width):
    for axis, dim in sides:
        size, length = (lax.axis_size(axis), x.shape[dim])
        up = [(i, (i + 1) % size) for i in range(size - 1)]
        down = [(j, i) for i, j in up]
        last = lax.slice_in_dim(x, length - width, length, axis=dim)
        first = lax.slice_in_dim(x, 0, width, axis=dim)
        before = lax.ppermute(last, axis, up)
        after = lax.ppermute(first, axis, down)
        x = jnp.concatenate([before, x, after], axis=dim)
    return x


def index_bits(axes):
    bits = []
    for axis in reversed(axes):
        size = lax.axis_size(axis)
        assert size & (size - 1) == 0
        bits += [(axis, b) for b in range(size.bit_length() - 1)]
    return bits


def exchange(x, axis, bit):
    size = lax.axis_size(axis)
    pairs = [(i, i ^ (1 << bit)) for i in range(size)]
    return lax.ppermute(x, axis, pairs)


def butterfly_sum(x, axes):
    for axis, bit in index_bits(axes):
        x = jax.tree.map(lambda v, w: v + w, x, exchange(x, axis, bit))
    return x


def halving_scatter(x, steps, bit_axes):
    bit_axes = list(bit_axes)
    for axis, bit, combined in steps:
        ax = bit_axes.index(combined)
        mine = (lax.axis_index(axis) >> bit) & 1
        keep = lax.dynamic_index_in_dim(x, mine, ax, keepdims=False)
        send = lax.dynamic_index_in_dim(x, 1 - mine, ax, keepdims=False)
        x = keep + exchange(send, axis, bit)
        bit_axes.pop(ax)
    return x


def body(
    features,
    conv_out,
    conv_weight,
    norm_gain_vector,
    norm_shift_vector,
    class_map,
    labels,
    class_weight,
):
    highest = lax.Precision.HIGHEST
    images, tile_rows, columns, in_chans = features.shape
    out_chans = conv_out.shape[3]
    taps = conv_weight.shape[0]
    local_pix = images * tile_rows * columns
    per_replica_part = IMG_DEV * H * W
    all_pix = lax.axis_size("rep") * per_replica_part
    classes = class_map.shape[0]

    onehot = (
        labels.reshape(local_pix, 1) == jnp.arange(classes, dtype=jnp.int32)
    ).astype(jnp.float32)
    weights_pix = jnp.sum(onehot * class_weight.astype(jnp.float32), -1)

    yvals = conv_out.astype(jnp.float32).reshape(local_pix, out_chans)
    first_sums = lax.psum(jnp.concatenate([jnp.sum(yvals, 0), jnp.sum(weights_pix)[None]]), "tile")
    column_sum, weight_tile = first_sums[:out_chans], first_sums[out_chans]
    weight_total = butterfly_sum(weight_tile, ("rep",))
    centre_offset = yvals - column_sum / per_replica_part
    variance = lax.psum(jnp.sum(centre_offset * centre_offset, 0), "tile") / per_replica_part
    inverse_deviation = lax.rsqrt(variance + 1e-05)
    normalized_input = centre_offset * inverse_deviation
    preactivation_values = norm_gain_vector * normalized_input + norm_shift_vector
    zvals = jnp.maximum(preactivation_values, 0.0)
    logits = jnp.dot(zvals, class_map.T, precision=highest)
    top_val = jnp.max(logits, -1, keepdims=True)
    log_total = top_val[:, 0] + jnp.log(jnp.sum(jnp.exp(logits - top_val), -1))
    cross = log_total - jnp.sum(onehot * logits, -1)
    mean_weight = weight_total / all_pix
    probs = jnp.exp(logits - log_total[:, None])
    grad_logit = (weights_pix / mean_weight)[:, None] * (probs - onehot)
    class_local_slice = jnp.dot(grad_logit.T, zvals, precision=highest)
    grad_z = jnp.dot(grad_logit, class_map, precision=highest)
    preactivation_gradient = jnp.where(preactivation_values > 0, grad_z, 0.0)
    first_gradient_sum, second_gradient_sum, class_tile, loss_tile = lax.psum(
        (
            jnp.sum(preactivation_gradient, 0),
            jnp.sum(preactivation_gradient * normalized_input, 0),
            class_local_slice,
            jnp.sum(weights_pix * cross),
        ),
        "tile",
    )
    packed = jnp.concatenate(
        [first_gradient_sum, second_gradient_sum, class_tile.reshape(-1), loss_tile[None]]
    )
    normalized_output_gradient = (
        norm_gain_vector
        * inverse_deviation
        * (
            preactivation_gradient
            - first_gradient_sum / per_replica_part
            - normalized_input * second_gradient_sum / per_replica_part
        )
    ).astype(jnp.bfloat16)
    normalized_output_gradient = normalized_output_gradient.reshape(
        images, tile_rows, columns, out_chans
    )
    extended = padded(normalized_output_gradient, (("tile", 1),), RATE)
    extended = jnp.pad(extended, ((0, 0), (0, 0), (RATE, RATE), (0, 0)))
    shifted_list = []
    for tap_index in range(taps):
        row_off = RATE - (tap_index // 3 - 1) * RATE
        col_off = RATE - (tap_index % 3 - 1) * RATE
        piece = extended[:, row_off : row_off + tile_rows, col_off : col_off + columns, :]
        shifted_list.append(piece.reshape(local_pix, out_chans))
    shifted = jnp.concatenate(shifted_list, 1)

    blocks = lax.axis_size("rep") * lax.axis_size("tile")
    nbits = blocks.bit_length() - 1
    rows = in_chans // blocks
    flat_x = features.reshape(local_pix, in_chans)
    packed, flat_x = lax.optimization_barrier((packed, flat_x))
    bits = [(axis, bit, combined) for combined, (axis, bit) in enumerate(index_bits(("rep", "tile")))]
    rest = bits[1:]
    orders = [rest, rest[1:] + rest[:1], rest[2:3] + rest[:2] + rest[3:]]
    group_taps = [taps - 2 * (taps // 3), taps // 3, taps // 3]
    starts = [sum(group_taps[:s]) for s in range(3)]
    parts = []
    for s in range(3):
        cols = shifted[:, starts[s] * out_chans : (starts[s] + group_taps[s]) * out_chans]
        part = lax.dot_general(
            flat_x, cols, (((0,), (0,)), ((), ())), preferred_element_type=jnp.float32
        )
        parts.append(part.reshape((2,) * nbits + (rows, group_taps[s] * out_chans)))

    halves = 2 if images % 2 == 0 else 1
    share = local_pix // halves
    grad_chunks = [
        lax.dot_general(
            shifted[h * share : (h + 1) * share].reshape(share, taps, out_chans),
            conv_weight,
            (((1, 2), (0, 2)), ((), ())),
            preferred_element_type=jnp.float32,
        ).astype(jnp.bfloat16)
        for h in range(halves)
    ]
    axis, bit, combined = bits[0]
    bit_axes = list(range(nbits - 1, -1, -1))
    ax = bit_axes.index(combined)
    mine = (lax.axis_index(axis) >> bit) & 1
    keeps = [lax.dynamic_index_in_dim(p, mine, ax, keepdims=False) for p in parts]
    sends = [lax.dynamic_index_in_dim(p, 1 - mine, ax, keepdims=False) for p in parts]
    received = lax.optimization_barrier([exchange(v, axis, bit) for v in sends])
    bit_axes.pop(ax)
    pieces = [keeps[s] + received[s] for s in range(3)]
    small_bits = index_bits(("rep",))
    axes_of = [list(bit_axes) for s in range(3)]
    for step in range(len(rest)):
        sends, keeps = [], []
        for s in range(3):
            axis, bit, combined = orders[s][step]
            ax = axes_of[s].index(combined)
            mine = (lax.axis_index(axis) >> bit) & 1
            keeps.append(lax.dynamic_index_in_dim(pieces[s], mine, ax, keepdims=False))
            sends.append(lax.dynamic_index_in_dim(pieces[s], 1 - mine, ax, keepdims=False))
            axes_of[s].pop(ax)
        received = []
        if step < len(small_bits):
            packed, sends = lax.optimization_barrier((packed, sends))
            received.append(exchange(packed, *small_bits[step]))
        received = [exchange(sends[s], orders[s][step][0], orders[s][step][1]) for s in range(3)] + received
        if step < halves:
            received, grad_chunks[step] = lax.optimization_barrier((received, grad_chunks[step]))
        else:
            received = lax.optimization_barrier(received)
        if step < len(small_bits):
            packed = packed + received.pop()
        pieces = [keeps[s] + received[s] for s in range(3)]
    grad_weight = jnp.concatenate(pieces, 1).reshape(rows, taps, out_chans)

    for step in range(len(rest), len(small_bits)):
        packed = packed + exchange(packed, *small_bits[step])
    grad_shift = packed[:out_chans]
    grad_gain = packed[out_chans : 2 * out_chans]
    grad_class = packed[2 * out_chans : (2 + classes) * out_chans].reshape(classes, out_chans)
    loss = packed[(2 + classes) * out_chans] / mean_weight / all_pix
    grad_features = jnp.concatenate(grad_chunks, 0).reshape(images, tile_rows, columns, in_chans)
    return (grad_features, grad_weight, grad_gain, grad_shift, grad_class, loss)


def solution(mesh):
    in_specs = (
        P("rep", "tile", None, None),
        P("rep", "tile", None, None),
        P(),
        P(),
        P(),
        P(),
        P("rep", "tile", None),
        P(),
    )
    out_specs = (P("rep", "tile", None, None), P(("rep", "tile"), None, None), P(), P(), P(), P())
    return jax.shard_map(body, mesh=mesh, in_specs=in_specs, out_specs=out_specs, check_vma=False)
```

```python
import jax
import jax.numpy as jnp
from jax import lax
from jax.sharding import PartitionSpec as P

IMG_DEV = 2
H = 48
W = 72
RATE = 12


def padded(x, sides, width):
    for axis, dim in sides:
        size, length = (lax.axis_size(axis), x.shape[dim])
        up = [(i, (i + 1) % size) for i in range(size - 1)]
        down = [(j, i) for i, j in up]
        last = lax.slice_in_dim(x, length - width, length, axis=dim)
        first = lax.slice_in_dim(x, 0, width, axis=dim)
        before = lax.ppermute(last, axis, up)
        after = lax.ppermute(first, axis, down)
        x = jnp.concatenate([before, x, after], axis=dim)
    return x


def index_bits(axes):
    bits = []
    for axis in reversed(axes):
        size = lax.axis_size(axis)
        assert size & (size - 1) == 0
        bits += [(axis, b) for b in range(size.bit_length() - 1)]
    return bits


def exchange(x, axis, bit):
    size = lax.axis_size(axis)
    pairs = [(i, i ^ (1 << bit)) for i in range(size)]
    return lax.ppermute(x, axis, pairs)


def butterfly_sum(x, axes):
    for axis, bit in index_bits(axes):
        x = jax.tree.map(lambda v, w: v + w, x, exchange(x, axis, bit))
    return x


def halving_scatter(x, steps, bit_axes):
    bit_axes = list(bit_axes)
    for axis, bit, combined in steps:
        ax = bit_axes.index(combined)
        mine = (lax.axis_index(axis) >> bit) & 1
        keep = lax.dynamic_index_in_dim(x, mine, ax, keepdims=False)
        send = lax.dynamic_index_in_dim(x, 1 - mine, ax, keepdims=False)
        x = keep + exchange(send, axis, bit)
        bit_axes.pop(ax)
    return x


def body(
    features,
    conv_out,
    conv_weight,
    norm_gain_vector,
    norm_shift_vector,
    class_map,
    labels,
    class_weight,
):
    highest = lax.Precision.HIGHEST
    images, tile_rows, columns, in_chans = features.shape
    out_chans = conv_out.shape[3]
    taps = conv_weight.shape[0]
    local_pix = images * tile_rows * columns
    per_replica_part = IMG_DEV * H * W
    all_pix = lax.axis_size("rep") * per_replica_part
    classes = class_map.shape[0]

    onehot = (
        labels.reshape(local_pix, 1) == jnp.arange(classes, dtype=jnp.int32)
    ).astype(jnp.float32)
    weights_pix = jnp.sum(onehot * class_weight.astype(jnp.float32), -1)

    yvals = conv_out.astype(jnp.float32).reshape(local_pix, out_chans)
    first_sums = lax.psum(jnp.concatenate([jnp.sum(yvals, 0), jnp.sum(weights_pix)[None]]), "tile")
    column_sum, weight_tile = first_sums[:out_chans], first_sums[out_chans]
    weight_total = butterfly_sum(weight_tile, ("rep",))
    centre_offset = yvals - column_sum / per_replica_part
    variance = lax.psum(jnp.sum(centre_offset * centre_offset, 0), "tile") / per_replica_part
    inverse_deviation = lax.rsqrt(variance + 1e-05)
    normalized_input = centre_offset * inverse_deviation
    preactivation_values = norm_gain_vector * normalized_input + norm_shift_vector
    zvals = jnp.maximum(preactivation_values, 0.0)
    logits = jnp.dot(zvals, class_map.T, precision=highest)
    top_val = jnp.max(logits, -1, keepdims=True)
    log_total = top_val[:, 0] + jnp.log(jnp.sum(jnp.exp(logits - top_val), -1))
    cross = log_total - jnp.sum(onehot * logits, -1)
    mean_weight = weight_total / all_pix
    probs = jnp.exp(logits - log_total[:, None])
    grad_logit = (weights_pix / mean_weight)[:, None] * (probs - onehot)
    class_local_slice = jnp.dot(grad_logit.T, zvals, precision=highest)
    grad_z = jnp.dot(grad_logit, class_map, precision=highest)
    preactivation_gradient = jnp.where(preactivation_values > 0, grad_z, 0.0)
    first_gradient_sum, second_gradient_sum, class_tile, loss_tile = lax.psum(
        (
            jnp.sum(preactivation_gradient, 0),
            jnp.sum(preactivation_gradient * normalized_input, 0),
            class_local_slice,
            jnp.sum(weights_pix * cross),
        ),
        "tile",
    )
    packed = jnp.concatenate(
        [first_gradient_sum, second_gradient_sum, class_tile.reshape(-1), loss_tile[None]]
    )
    normalized_output_gradient = (
        norm_gain_vector
        * inverse_deviation
        * (
            preactivation_gradient
            - first_gradient_sum / per_replica_part
            - normalized_input * second_gradient_sum / per_replica_part
        )
    ).astype(jnp.bfloat16)
    normalized_output_gradient = normalized_output_gradient.reshape(
        images, tile_rows, columns, out_chans
    )
    column_pad = ((0, 0), (0, 0), (RATE, RATE), (0, 0))
    extended = jnp.pad(padded(normalized_output_gradient, (("tile", 1),), RATE), column_pad)
    own_rows = jnp.pad(normalized_output_gradient, column_pad)
    shifted_list = []
    for tap_index in range(taps):
        row_off = RATE - (tap_index // 3 - 1) * RATE
        col_off = RATE - (tap_index % 3 - 1) * RATE
        if tap_index // 3 == 1:
            piece = own_rows[:, :, col_off : col_off + columns, :]
        else:
            piece = extended[:, row_off : row_off + tile_rows, col_off : col_off + columns, :]
        shifted_list.append(piece.reshape(local_pix, out_chans))
    shifted = jnp.concatenate(shifted_list, 1)

    blocks = lax.axis_size("rep") * lax.axis_size("tile")
    nbits = blocks.bit_length() - 1
    rows = in_chans // blocks
    flat_x = features.reshape(local_pix, in_chans)
    packed, flat_x = lax.optimization_barrier((packed, flat_x))
    bits = [(axis, bit, combined) for combined, (axis, bit) in enumerate(index_bits(("rep", "tile")))]
    rest = bits[1:]
    orders = [rest, rest[1:] + rest[:1], rest[2:3] + rest[:2] + rest[3:]]
    group_taps = [taps - 2 * (taps // 3), taps // 3, taps // 3]
    starts = [sum(group_taps[:s]) for s in range(3)]
    parts = []
    for s in range(3):
        cols = jnp.concatenate(shifted_list[starts[s] : starts[s] + group_taps[s]], 1)
        part = lax.dot_general(
            flat_x, cols, (((0,), (0,)), ((), ())), preferred_element_type=jnp.float32
        )
        parts.append(part.reshape((2,) * nbits + (rows, group_taps[s] * out_chans)))

    halves = 2 if images % 2 == 0 else 1
    share = local_pix // halves
    grad_chunks = [
        lax.dot_general(
            shifted[h * share : (h + 1) * share].reshape(share, taps, out_chans),
            conv_weight,
            (((1, 2), (0, 2)), ((), ())),
            preferred_element_type=jnp.float32,
        ).astype(jnp.bfloat16)
        for h in range(halves)
    ]
    axis, bit, combined = bits[0]
    bit_axes = list(range(nbits - 1, -1, -1))
    ax = bit_axes.index(combined)
    mine = (lax.axis_index(axis) >> bit) & 1
    keeps = [lax.dynamic_index_in_dim(p, mine, ax, keepdims=False) for p in parts]
    sends = [lax.dynamic_index_in_dim(p, 1 - mine, ax, keepdims=False) for p in parts]
    received = lax.optimization_barrier([exchange(v, axis, bit) for v in sends])
    bit_axes.pop(ax)
    pieces = [keeps[s] + received[s] for s in range(3)]
    small_bits = index_bits(("rep",))
    axes_of = [list(bit_axes) for s in range(3)]
    for step in range(len(rest)):
        sends, keeps = [], []
        for s in range(3):
            axis, bit, combined = orders[s][step]
            ax = axes_of[s].index(combined)
            mine = (lax.axis_index(axis) >> bit) & 1
            keeps.append(lax.dynamic_index_in_dim(pieces[s], mine, ax, keepdims=False))
            sends.append(lax.dynamic_index_in_dim(pieces[s], 1 - mine, ax, keepdims=False))
            axes_of[s].pop(ax)
        received = []
        if step < len(small_bits):
            packed, sends = lax.optimization_barrier((packed, sends))
            received.append(exchange(packed, *small_bits[step]))
        received = [exchange(sends[s], orders[s][step][0], orders[s][step][1]) for s in range(3)] + received
        if step < halves:
            received, grad_chunks[step] = lax.optimization_barrier((received, grad_chunks[step]))
        else:
            received = lax.optimization_barrier(received)
        if step < len(small_bits):
            packed = packed + received.pop()
        pieces = [keeps[s] + received[s] for s in range(3)]
    grad_weight = jnp.concatenate(pieces, 1).reshape(rows, taps, out_chans)

    for step in range(len(rest), len(small_bits)):
        packed = packed + exchange(packed, *small_bits[step])
    grad_shift = packed[:out_chans]
    grad_gain = packed[out_chans : 2 * out_chans]
    grad_class = packed[2 * out_chans : (2 + classes) * out_chans].reshape(classes, out_chans)
    loss = packed[(2 + classes) * out_chans] / mean_weight / all_pix
    grad_features = jnp.concatenate(grad_chunks, 0).reshape(images, tile_rows, columns, in_chans)
    return (grad_features, grad_weight, grad_gain, grad_shift, grad_class, loss)


def solution(mesh):
    in_specs = (
        P("rep", "tile", None, None),
        P("rep", "tile", None, None),
        P(),
        P(),
        P(),
        P(),
        P("rep", "tile", None),
        P(),
    )
    out_specs = (P("rep", "tile", None, None), P(("rep", "tile"), None, None), P(), P(), P(), P())
    return jax.shard_map(body, mesh=mesh, in_specs=in_specs, out_specs=out_specs, check_vma=False)
```

```python
import jax
import jax.numpy as jnp
from jax import lax
from jax.sharding import PartitionSpec as P

IMG_DEV = 2
H = 48
W = 72
RATE = 12


def padded(x, sides, width):
    for axis, dim in sides:
        size, length = (lax.axis_size(axis), x.shape[dim])
        up = [(i, (i + 1) % size) for i in range(size - 1)]
        down = [(j, i) for i, j in up]
        last = lax.slice_in_dim(x, length - width, length, axis=dim)
        first = lax.slice_in_dim(x, 0, width, axis=dim)
        before = lax.ppermute(last, axis, up)
        after = lax.ppermute(first, axis, down)
        x = jnp.concatenate([before, x, after], axis=dim)
    return x


def index_bits(axes):
    bits = []
    for axis in reversed(axes):
        size = lax.axis_size(axis)
        assert size & (size - 1) == 0
        bits += [(axis, b) for b in range(size.bit_length() - 1)]
    return bits


def exchange(x, axis, bit):
    size = lax.axis_size(axis)
    pairs = [(i, i ^ (1 << bit)) for i in range(size)]
    return lax.ppermute(x, axis, pairs)


def butterfly_sum(x, axes):
    for axis, bit in index_bits(axes):
        x = jax.tree.map(lambda v, w: v + w, x, exchange(x, axis, bit))
    return x


def halving_scatter(x, steps, bit_axes):
    bit_axes = list(bit_axes)
    for axis, bit, combined in steps:
        ax = bit_axes.index(combined)
        mine = (lax.axis_index(axis) >> bit) & 1
        keep = lax.dynamic_index_in_dim(x, mine, ax, keepdims=False)
        send = lax.dynamic_index_in_dim(x, 1 - mine, ax, keepdims=False)
        x = keep + exchange(send, axis, bit)
        bit_axes.pop(ax)
    return x


def body(
    features,
    conv_out,
    conv_weight,
    norm_gain_vector,
    norm_shift_vector,
    class_map,
    labels,
    class_weight,
):
    highest = lax.Precision.HIGHEST
    images, tile_rows, columns, in_chans = features.shape
    out_chans = conv_out.shape[3]
    taps = conv_weight.shape[0]
    local_pix = images * tile_rows * columns
    per_replica_part = IMG_DEV * H * W
    all_pix = lax.axis_size("rep") * per_replica_part
    classes = class_map.shape[0]

    onehot = (
        labels.reshape(local_pix, 1) == jnp.arange(classes, dtype=jnp.int32)
    ).astype(jnp.float32)
    weights_pix = jnp.sum(onehot * class_weight.astype(jnp.float32), -1)

    yvals = conv_out.astype(jnp.float32).reshape(local_pix, out_chans)
    first_sums = lax.psum(jnp.concatenate([jnp.sum(yvals, 0), jnp.sum(weights_pix)[None]]), "tile")
    column_sum, weight_tile = first_sums[:out_chans], first_sums[out_chans]
    weight_total = butterfly_sum(weight_tile, ("rep",))
    centre_offset = yvals - column_sum / per_replica_part
    variance = lax.psum(jnp.sum(centre_offset * centre_offset, 0), "tile") / per_replica_part
    inverse_deviation = lax.rsqrt(variance + 1e-05)
    normalized_input = centre_offset * inverse_deviation
    preactivation_values = norm_gain_vector * normalized_input + norm_shift_vector
    zvals = jnp.maximum(preactivation_values, 0.0)
    logits = jnp.dot(zvals, class_map.T, precision=highest)
    top_val = jnp.max(logits, -1, keepdims=True)
    log_total = top_val[:, 0] + jnp.log(jnp.sum(jnp.exp(logits - top_val), -1))
    cross = log_total - jnp.sum(onehot * logits, -1)
    mean_weight = weight_total / all_pix
    probs = jnp.exp(logits - log_total[:, None])
    grad_logit = (weights_pix / mean_weight)[:, None] * (probs - onehot)
    class_local_slice = jnp.dot(grad_logit.T, zvals, precision=highest)
    grad_z = jnp.dot(grad_logit, class_map, precision=highest)
    preactivation_gradient = jnp.where(preactivation_values > 0, grad_z, 0.0)
    first_gradient_sum, second_gradient_sum, class_tile, loss_tile = lax.psum(
        (
            jnp.sum(preactivation_gradient, 0),
            jnp.sum(preactivation_gradient * normalized_input, 0),
            class_local_slice,
            jnp.sum(weights_pix * cross),
        ),
        "tile",
    )
    packed = jnp.concatenate(
        [first_gradient_sum, second_gradient_sum, class_tile.reshape(-1), loss_tile[None]]
    )
    normalized_output_gradient = (
        norm_gain_vector
        * inverse_deviation
        * (
            preactivation_gradient
            - first_gradient_sum / per_replica_part
            - normalized_input * second_gradient_sum / per_replica_part
        )
    ).astype(jnp.bfloat16)
    normalized_output_gradient = normalized_output_gradient.reshape(
        images, tile_rows, columns, out_chans
    )
    column_pad = ((0, 0), (0, 0), (RATE, RATE), (0, 0))
    extended = jnp.pad(padded(normalized_output_gradient, (("tile", 1),), RATE), column_pad)
    own_rows = jnp.pad(normalized_output_gradient, column_pad)
    shifted_list = []
    for tap_index in range(taps):
        row_off = RATE - (tap_index // 3 - 1) * RATE
        col_off = RATE - (tap_index % 3 - 1) * RATE
        if tap_index // 3 == 1:
            piece = own_rows[:, :, col_off : col_off + columns, :]
        else:
            piece = extended[:, row_off : row_off + tile_rows, col_off : col_off + columns, :]
        shifted_list.append(piece.reshape(local_pix, out_chans))
    shifted = jnp.concatenate(shifted_list, 1)

    blocks = lax.axis_size("rep") * lax.axis_size("tile")
    nbits = blocks.bit_length() - 1
    rows = in_chans // blocks
    flat_x = features.reshape(local_pix, in_chans)
    packed, flat_x = lax.optimization_barrier((packed, flat_x))
    bits = [(axis, bit, combined) for combined, (axis, bit) in enumerate(index_bits(("rep", "tile")))]
    rest = bits[1:]
    orders = [rest, rest[1:] + rest[:1], rest[2:3] + rest[:2] + rest[3:]]
    group_taps = [taps - 2 * (taps // 3), taps // 3, taps // 3]
    starts = [sum(group_taps[:s]) for s in range(3)]
    parts = []
    for s in range(3):
        cols = jnp.concatenate(shifted_list[starts[s] : starts[s] + group_taps[s]], 1)
        part = lax.dot_general(
            flat_x, cols, (((0,), (0,)), ((), ())), preferred_element_type=jnp.float32
        )
        parts.append(part.reshape((2,) * nbits + (rows, group_taps[s] * out_chans)))

    halves = 2
    share = in_chans // halves
    grad_chunks = [
        lax.dot_general(
            shifted.reshape(local_pix, taps, out_chans),
            conv_weight[:, h * share : (h + 1) * share, :],
            (((1, 2), (0, 2)), ((), ())),
            preferred_element_type=jnp.float32,
        ).astype(jnp.bfloat16)
        for h in range(halves)
    ]
    axis, bit, combined = bits[0]
    bit_axes = list(range(nbits - 1, -1, -1))
    ax = bit_axes.index(combined)
    mine = (lax.axis_index(axis) >> bit) & 1
    keeps = [lax.dynamic_index_in_dim(p, mine, ax, keepdims=False) for p in parts]
    sends = [lax.dynamic_index_in_dim(p, 1 - mine, ax, keepdims=False) for p in parts]
    received = lax.optimization_barrier([exchange(v, axis, bit) for v in sends])
    bit_axes.pop(ax)
    pieces = [keeps[s] + received[s] for s in range(3)]
    small_bits = index_bits(("rep",))
    axes_of = [list(bit_axes) for s in range(3)]
    for step in range(len(rest)):
        sends, keeps = [], []
        for s in range(3):
            axis, bit, combined = orders[s][step]
            ax = axes_of[s].index(combined)
            mine = (lax.axis_index(axis) >> bit) & 1
            keeps.append(lax.dynamic_index_in_dim(pieces[s], mine, ax, keepdims=False))
            sends.append(lax.dynamic_index_in_dim(pieces[s], 1 - mine, ax, keepdims=False))
            axes_of[s].pop(ax)
        received = []
        if step < len(small_bits):
            packed, sends = lax.optimization_barrier((packed, sends))
            received.append(exchange(packed, *small_bits[step]))
        received = [exchange(sends[s], orders[s][step][0], orders[s][step][1]) for s in range(3)] + received
        if step < halves:
            received, grad_chunks[step] = lax.optimization_barrier((received, grad_chunks[step]))
        else:
            received = lax.optimization_barrier(received)
        if step < len(small_bits):
            packed = packed + received.pop()
        pieces = [keeps[s] + received[s] for s in range(3)]
    grad_weight = jnp.concatenate(pieces, 1).reshape(rows, taps, out_chans)

    for step in range(len(rest), len(small_bits)):
        packed = packed + exchange(packed, *small_bits[step])
    grad_shift = packed[:out_chans]
    grad_gain = packed[out_chans : 2 * out_chans]
    grad_class = packed[2 * out_chans : (2 + classes) * out_chans].reshape(classes, out_chans)
    loss = packed[(2 + classes) * out_chans] / mean_weight / all_pix
    grad_features = jnp.concatenate(grad_chunks, 1).reshape(images, tile_rows, columns, in_chans)
    return (grad_features, grad_weight, grad_gain, grad_shift, grad_class, loss)


def solution(mesh):
    in_specs = (
        P("rep", "tile", None, None),
        P("rep", "tile", None, None),
        P(),
        P(),
        P(),
        P(),
        P("rep", "tile", None),
        P(),
    )
    out_specs = (P("rep", "tile", None, None), P(("rep", "tile"), None, None), P(), P(), P(), P())
    return jax.shard_map(body, mesh=mesh, in_specs=in_specs, out_specs=out_specs, check_vma=False)
```

```python
import jax
import jax.numpy as jnp
from jax import lax
from jax.sharding import PartitionSpec as P

IMG_DEV = 2
H = 48
W = 72
RATE = 12


def padded(x, sides, width):
    for axis, dim in sides:
        size, length = (lax.axis_size(axis), x.shape[dim])
        up = [(i, (i + 1) % size) for i in range(size - 1)]
        down = [(j, i) for i, j in up]
        last = lax.slice_in_dim(x, length - width, length, axis=dim)
        first = lax.slice_in_dim(x, 0, width, axis=dim)
        before = lax.ppermute(last, axis, up)
        after = lax.ppermute(first, axis, down)
        x = jnp.concatenate([before, x, after], axis=dim)
    return x


def index_bits(axes):
    bits = []
    for axis in reversed(axes):
        size = lax.axis_size(axis)
        assert size & (size - 1) == 0
        bits += [(axis, b) for b in range(size.bit_length() - 1)]
    return bits


def exchange(x, axis, bit):
    size = lax.axis_size(axis)
    pairs = [(i, i ^ (1 << bit)) for i in range(size)]
    return lax.ppermute(x, axis, pairs)


def butterfly_sum(x, axes):
    for axis, bit in index_bits(axes):
        x = jax.tree.map(lambda v, w: v + w, x, exchange(x, axis, bit))
    return x


def halving_scatter(x, steps, bit_axes):
    bit_axes = list(bit_axes)
    for axis, bit, combined in steps:
        ax = bit_axes.index(combined)
        mine = (lax.axis_index(axis) >> bit) & 1
        keep = lax.dynamic_index_in_dim(x, mine, ax, keepdims=False)
        send = lax.dynamic_index_in_dim(x, 1 - mine, ax, keepdims=False)
        x = keep + exchange(send, axis, bit)
        bit_axes.pop(ax)
    return x


def body(
    features,
    conv_out,
    conv_weight,
    norm_gain_vector,
    norm_shift_vector,
    class_map,
    labels,
    class_weight,
):
    highest = lax.Precision.HIGHEST
    images, tile_rows, columns, in_chans = features.shape
    out_chans = conv_out.shape[3]
    taps = conv_weight.shape[0]
    local_pix = images * tile_rows * columns
    per_replica_part = IMG_DEV * H * W
    all_pix = lax.axis_size("rep") * per_replica_part
    classes = class_map.shape[0]

    onehot = (
        labels.reshape(local_pix, 1) == jnp.arange(classes, dtype=jnp.int32)
    ).astype(jnp.float32)
    weights_pix = jnp.sum(onehot * class_weight.astype(jnp.float32), -1)

    yvals = conv_out.astype(jnp.float32).reshape(local_pix, out_chans)
    tiles = lax.axis_size("tile")
    local_sum = jnp.sum(yvals, 0)
    local_offset = yvals - local_sum / local_pix
    local_stats = jnp.concatenate(
        [local_sum, jnp.sum(local_offset * local_offset, 0), jnp.sum(weights_pix)[None]]
    )
    slot = (jnp.arange(tiles) == lax.axis_index("tile")).astype(jnp.float32)
    tile_stats = lax.psum(slot[:, None] * local_stats[None, :], "tile")
    tile_sums = tile_stats[:, :out_chans]
    column_sum = jnp.sum(tile_sums, 0)
    tile_means = tile_sums / local_pix - column_sum / per_replica_part
    variance = (
        jnp.sum(tile_stats[:, out_chans : 2 * out_chans] + local_pix * tile_means * tile_means, 0)
        / per_replica_part
    )
    weight_total = butterfly_sum(jnp.sum(tile_stats[:, 2 * out_chans]), ("rep",))
    centre_offset = yvals - column_sum / per_replica_part
    inverse_deviation = lax.rsqrt(variance + 1e-05)
    normalized_input = centre_offset * inverse_deviation
    preactivation_values = norm_gain_vector * normalized_input + norm_shift_vector
    zvals = jnp.maximum(preactivation_values, 0.0)
    logits = jnp.dot(zvals, class_map.T, precision=highest)
    top_val = jnp.max(logits, -1, keepdims=True)
    log_total = top_val[:, 0] + jnp.log(jnp.sum(jnp.exp(logits - top_val), -1))
    cross = log_total - jnp.sum(onehot * logits, -1)
    mean_weight = weight_total / all_pix
    probs = jnp.exp(logits - log_total[:, None])
    grad_logit = (weights_pix / mean_weight)[:, None] * (probs - onehot)
    class_local_slice = jnp.dot(grad_logit.T, zvals, precision=highest)
    grad_z = jnp.dot(grad_logit, class_map, precision=highest)
    preactivation_gradient = jnp.where(preactivation_values > 0, grad_z, 0.0)
    first_gradient_sum, second_gradient_sum, class_tile, loss_tile = lax.psum(
        (
            jnp.sum(preactivation_gradient, 0),
            jnp.sum(preactivation_gradient * normalized_input, 0),
            class_local_slice,
            jnp.sum(weights_pix * cross),
        ),
        "tile",
    )
    packed = jnp.concatenate(
        [first_gradient_sum, second_gradient_sum, class_tile.reshape(-1), loss_tile[None]]
    )
    normalized_output_gradient = (
        norm_gain_vector
        * inverse_deviation
        * (
            preactivation_gradient
            - first_gradient_sum / per_replica_part
            - normalized_input * second_gradient_sum / per_replica_part
        )
    ).astype(jnp.bfloat16)
    normalized_output_gradient = normalized_output_gradient.reshape(
        images, tile_rows, columns, out_chans
    )
    column_pad = ((0, 0), (0, 0), (RATE, RATE), (0, 0))
    extended = jnp.pad(padded(normalized_output_gradient, (("tile", 1),), RATE), column_pad)
    own_rows = jnp.pad(normalized_output_gradient, column_pad)
    shifted_list = []
    for tap_index in range(taps):
        row_off = RATE - (tap_index // 3 - 1) * RATE
        col_off = RATE - (tap_index % 3 - 1) * RATE
        if tap_index // 3 == 1:
            piece = own_rows[:, :, col_off : col_off + columns, :]
        else:
            piece = extended[:, row_off : row_off + tile_rows, col_off : col_off + columns, :]
        shifted_list.append(piece.reshape(local_pix, out_chans))
    shifted = jnp.concatenate(shifted_list, 1)

    blocks = lax.axis_size("rep") * lax.axis_size("tile")
    nbits = blocks.bit_length() - 1
    rows = in_chans // blocks
    flat_x = features.reshape(local_pix, in_chans)
    packed, flat_x = lax.optimization_barrier((packed, flat_x))
    bits = [(axis, bit, combined) for combined, (axis, bit) in enumerate(index_bits(("rep", "tile")))]
    rest = bits[1:]
    orders = [rest, rest[1:] + rest[:1], rest[2:3] + rest[:2] + rest[3:]]
    group_taps = [taps - 2 * (taps // 3), taps // 3, taps // 3]
    starts = [sum(group_taps[:s]) for s in range(3)]
    parts = []
    for s in range(3):
        cols = jnp.concatenate(shifted_list[starts[s] : starts[s] + group_taps[s]], 1)
        part = lax.dot_general(
            flat_x, cols, (((0,), (0,)), ((), ())), preferred_element_type=jnp.float32
        )
        parts.append(part.reshape((2,) * nbits + (rows, group_taps[s] * out_chans)))

    halves = 2
    share = in_chans // halves
    grad_chunks = [
        lax.dot_general(
            shifted.reshape(local_pix, taps, out_chans),
            conv_weight[:, h * share : (h + 1) * share, :],
            (((1, 2), (0, 2)), ((), ())),
            preferred_element_type=jnp.float32,
        ).astype(jnp.bfloat16)
        for h in range(halves)
    ]
    axis, bit, combined = bits[0]
    bit_axes = list(range(nbits - 1, -1, -1))
    ax = bit_axes.index(combined)
    mine = (lax.axis_index(axis) >> bit) & 1
    keeps = [lax.dynamic_index_in_dim(p, mine, ax, keepdims=False) for p in parts]
    sends = [lax.dynamic_index_in_dim(p, 1 - mine, ax, keepdims=False) for p in parts]
    received = lax.optimization_barrier([exchange(v, axis, bit) for v in sends])
    bit_axes.pop(ax)
    pieces = [keeps[s] + received[s] for s in range(3)]
    small_bits = index_bits(("rep",))
    axes_of = [list(bit_axes) for s in range(3)]
    for step in range(len(rest)):
        sends, keeps = [], []
        for s in range(3):
            axis, bit, combined = orders[s][step]
            ax = axes_of[s].index(combined)
            mine = (lax.axis_index(axis) >> bit) & 1
            keeps.append(lax.dynamic_index_in_dim(pieces[s], mine, ax, keepdims=False))
            sends.append(lax.dynamic_index_in_dim(pieces[s], 1 - mine, ax, keepdims=False))
            axes_of[s].pop(ax)
        received = []
        if step < len(small_bits):
            packed, sends = lax.optimization_barrier((packed, sends))
            received.append(exchange(packed, *small_bits[step]))
        received = [exchange(sends[s], orders[s][step][0], orders[s][step][1]) for s in range(3)] + received
        if step < halves:
            received, grad_chunks[step] = lax.optimization_barrier((received, grad_chunks[step]))
        else:
            received = lax.optimization_barrier(received)
        if step < len(small_bits):
            packed = packed + received.pop()
        pieces = [keeps[s] + received[s] for s in range(3)]
    grad_weight = jnp.concatenate(pieces, 1).reshape(rows, taps, out_chans)

    for step in range(len(rest), len(small_bits)):
        packed = packed + exchange(packed, *small_bits[step])
    grad_shift = packed[:out_chans]
    grad_gain = packed[out_chans : 2 * out_chans]
    grad_class = packed[2 * out_chans : (2 + classes) * out_chans].reshape(classes, out_chans)
    loss = packed[(2 + classes) * out_chans] / mean_weight / all_pix
    grad_features = jnp.concatenate(grad_chunks, 1).reshape(images, tile_rows, columns, in_chans)
    return (grad_features, grad_weight, grad_gain, grad_shift, grad_class, loss)


def solution(mesh):
    in_specs = (
        P("rep", "tile", None, None),
        P("rep", "tile", None, None),
        P(),
        P(),
        P(),
        P(),
        P("rep", "tile", None),
        P(),
    )
    out_specs = (P("rep", "tile", None, None), P(("rep", "tile"), None, None), P(), P(), P(), P())
    return jax.shard_map(body, mesh=mesh, in_specs=in_specs, out_specs=out_specs, check_vma=False)
```

```python
import jax
import jax.numpy as jnp
from jax import lax
from jax.sharding import PartitionSpec as P

IMG_DEV = 2
H = 48
W = 72
RATE = 12


def padded(x, sides, width):
    for axis, dim in sides:
        size, length = (lax.axis_size(axis), x.shape[dim])
        up = [(i, (i + 1) % size) for i in range(size - 1)]
        down = [(j, i) for i, j in up]
        last = lax.slice_in_dim(x, length - width, length, axis=dim)
        first = lax.slice_in_dim(x, 0, width, axis=dim)
        before = lax.ppermute(last, axis, up)
        after = lax.ppermute(first, axis, down)
        x = jnp.concatenate([before, x, after], axis=dim)
    return x


def index_bits(axes):
    bits = []
    for axis in reversed(axes):
        size = lax.axis_size(axis)
        assert size & (size - 1) == 0
        bits += [(axis, b) for b in range(size.bit_length() - 1)]
    return bits


def exchange(x, axis, bit):
    size = lax.axis_size(axis)
    pairs = [(i, i ^ (1 << bit)) for i in range(size)]
    return lax.ppermute(x, axis, pairs)


def butterfly_sum(x, axes):
    for axis, bit in index_bits(axes):
        x = jax.tree.map(lambda v, w: v + w, x, exchange(x, axis, bit))
    return x


def halving_scatter(x, steps, bit_axes):
    bit_axes = list(bit_axes)
    for axis, bit, combined in steps:
        ax = bit_axes.index(combined)
        mine = (lax.axis_index(axis) >> bit) & 1
        keep = lax.dynamic_index_in_dim(x, mine, ax, keepdims=False)
        send = lax.dynamic_index_in_dim(x, 1 - mine, ax, keepdims=False)
        x = keep + exchange(send, axis, bit)
        bit_axes.pop(ax)
    return x


def body(
    features,
    conv_out,
    conv_weight,
    norm_gain_vector,
    norm_shift_vector,
    class_map,
    labels,
    class_weight,
):
    highest = lax.Precision.HIGHEST
    images, tile_rows, columns, in_chans = features.shape
    out_chans = conv_out.shape[3]
    taps = conv_weight.shape[0]
    local_pix = images * tile_rows * columns
    per_replica_part = IMG_DEV * H * W
    all_pix = lax.axis_size("rep") * per_replica_part
    classes = class_map.shape[0]

    onehot = (
        labels.reshape(local_pix, 1) == jnp.arange(classes, dtype=jnp.int32)
    ).astype(jnp.float32)
    weights_pix = jnp.sum(onehot * class_weight.astype(jnp.float32), -1)

    yvals = conv_out.astype(jnp.float32).reshape(local_pix, out_chans)
    tiles = lax.axis_size("tile")
    local_sum = jnp.sum(yvals, 0)
    local_offset = yvals - local_sum / local_pix
    local_stats = jnp.concatenate(
        [local_sum, jnp.sum(local_offset * local_offset, 0), jnp.sum(weights_pix)[None]]
    )
    slot = (jnp.arange(tiles) == lax.axis_index("tile")).astype(jnp.float32)
    tile_stats = lax.psum(slot[:, None] * local_stats[None, :], "tile")
    tile_sums = tile_stats[:, :out_chans]
    column_sum = jnp.sum(tile_sums, 0)
    tile_means = tile_sums / local_pix - column_sum / per_replica_part
    variance = (
        jnp.sum(tile_stats[:, out_chans : 2 * out_chans] + local_pix * tile_means * tile_means, 0)
        / per_replica_part
    )
    weight_total = butterfly_sum(jnp.sum(tile_stats[:, 2 * out_chans]), ("rep",))
    centre_offset = yvals - column_sum / per_replica_part
    inverse_deviation = lax.rsqrt(variance + 1e-05)
    normalized_input = centre_offset * inverse_deviation
    preactivation_values = norm_gain_vector * normalized_input + norm_shift_vector
    zvals = jnp.maximum(preactivation_values, 0.0)
    logits = jnp.dot(zvals, class_map.T, precision=highest)
    top_val = jnp.max(logits, -1, keepdims=True)
    log_total = top_val[:, 0] + jnp.log(jnp.sum(jnp.exp(logits - top_val), -1))
    cross = log_total - jnp.sum(onehot * logits, -1)
    mean_weight = weight_total / all_pix
    probs = jnp.exp(logits - log_total[:, None])
    grad_logit = (weights_pix / mean_weight)[:, None] * (probs - onehot)
    class_local_slice = jnp.dot(grad_logit.T, zvals, precision=highest)
    grad_z = jnp.dot(grad_logit, class_map, precision=highest)
    preactivation_gradient = jnp.where(preactivation_values > 0, grad_z, 0.0)
    first_gradient_sum, second_gradient_sum, class_tile, loss_tile = lax.psum(
        (
            jnp.sum(preactivation_gradient, 0),
            jnp.sum(preactivation_gradient * normalized_input, 0),
            class_local_slice,
            jnp.sum(weights_pix * cross),
        ),
        "tile",
    )
    packed = jnp.concatenate(
        [first_gradient_sum, second_gradient_sum, class_tile.reshape(-1), loss_tile[None]]
    )
    normalized_output_gradient = (
        norm_gain_vector
        * inverse_deviation
        * (
            preactivation_gradient
            - first_gradient_sum / per_replica_part
            - normalized_input * second_gradient_sum / per_replica_part
        )
    ).astype(jnp.bfloat16)
    normalized_output_gradient = normalized_output_gradient.reshape(
        images, tile_rows, columns, out_chans
    )
    column_pad = ((0, 0), (0, 0), (RATE, RATE), (0, 0))
    extended = jnp.pad(padded(normalized_output_gradient, (("tile", 1),), RATE), column_pad)
    own_rows = jnp.pad(normalized_output_gradient, column_pad)
    shifted_list = []
    for tap_index in range(taps):
        row_off = RATE - (tap_index // 3 - 1) * RATE
        col_off = RATE - (tap_index % 3 - 1) * RATE
        if tap_index // 3 == 1:
            piece = own_rows[:, :, col_off : col_off + columns, :]
        else:
            piece = extended[:, row_off : row_off + tile_rows, col_off : col_off + columns, :]
        shifted_list.append(piece.reshape(local_pix, out_chans))
    shifted = jnp.concatenate(shifted_list, 1)

    blocks = lax.axis_size("rep") * lax.axis_size("tile")
    nbits = blocks.bit_length() - 1
    rows = in_chans // blocks
    flat_x = features.reshape(local_pix, in_chans)
    packed, flat_x = lax.optimization_barrier((packed, flat_x))
    bits = [(axis, bit, combined) for combined, (axis, bit) in enumerate(index_bits(("rep", "tile")))]
    rest = bits[1:]
    orders = [rest, rest[1:] + rest[:1], rest[2:3] + rest[:2] + rest[3:]]
    group_taps = [taps - 2 * (taps // 3), taps // 3, taps // 3]
    starts = [sum(group_taps[:s]) for s in range(3)]
    parts = []
    for s in range(3):
        cols = jnp.concatenate(shifted_list[starts[s] : starts[s] + group_taps[s]], 1)
        part = lax.dot_general(
            flat_x, cols, (((0,), (0,)), ((), ())), preferred_element_type=jnp.float32
        )
        parts.append(part.reshape((2,) * nbits + (rows, group_taps[s] * out_chans)))

    halves = 3
    share = in_chans // halves
    under = {0: [0, 1], 2: [2]}
    grad_chunks = [
        lax.dot_general(
            shifted.reshape(local_pix, taps, out_chans),
            conv_weight[:, h * share : (h + 1) * share, :],
            (((1, 2), (0, 2)), ((), ())),
            preferred_element_type=jnp.float32,
        ).astype(jnp.bfloat16)
        for h in range(halves)
    ]
    axis, bit, combined = bits[0]
    bit_axes = list(range(nbits - 1, -1, -1))
    ax = bit_axes.index(combined)
    mine = (lax.axis_index(axis) >> bit) & 1
    keeps = [lax.dynamic_index_in_dim(p, mine, ax, keepdims=False) for p in parts]
    sends = [lax.dynamic_index_in_dim(p, 1 - mine, ax, keepdims=False) for p in parts]
    received = lax.optimization_barrier([exchange(v, axis, bit) for v in sends])
    bit_axes.pop(ax)
    pieces = [keeps[s] + received[s] for s in range(3)]
    small_bits = index_bits(("rep",))
    axes_of = [list(bit_axes) for s in range(3)]
    for step in range(len(rest)):
        sends, keeps = [], []
        for s in range(3):
            axis, bit, combined = orders[s][step]
            ax = axes_of[s].index(combined)
            mine = (lax.axis_index(axis) >> bit) & 1
            keeps.append(lax.dynamic_index_in_dim(pieces[s], mine, ax, keepdims=False))
            sends.append(lax.dynamic_index_in_dim(pieces[s], 1 - mine, ax, keepdims=False))
            axes_of[s].pop(ax)
        received = []
        if step < len(small_bits):
            packed, sends = lax.optimization_barrier((packed, sends))
            received.append(exchange(packed, *small_bits[step]))
        received = [exchange(sends[s], orders[s][step][0], orders[s][step][1]) for s in range(3)] + received
        if step in under:
            covered = [grad_chunks[i] for i in under[step]]
            received, covered = lax.optimization_barrier((received, covered))
            for i, chunk in zip(under[step], covered):
                grad_chunks[i] = chunk
        else:
            received = lax.optimization_barrier(received)
        if step < len(small_bits):
            packed = packed + received.pop()
        pieces = [keeps[s] + received[s] for s in range(3)]
    grad_weight = jnp.concatenate(pieces, 1).reshape(rows, taps, out_chans)

    for step in range(len(rest), len(small_bits)):
        packed = packed + exchange(packed, *small_bits[step])
    grad_shift = packed[:out_chans]
    grad_gain = packed[out_chans : 2 * out_chans]
    grad_class = packed[2 * out_chans : (2 + classes) * out_chans].reshape(classes, out_chans)
    loss = packed[(2 + classes) * out_chans] / mean_weight / all_pix
    grad_features = jnp.concatenate(grad_chunks, 1).reshape(images, tile_rows, columns, in_chans)
    return (grad_features, grad_weight, grad_gain, grad_shift, grad_class, loss)


def solution(mesh):
    in_specs = (
        P("rep", "tile", None, None),
        P("rep", "tile", None, None),
        P(),
        P(),
        P(),
        P(),
        P("rep", "tile", None),
        P(),
    )
    out_specs = (P("rep", "tile", None, None), P(("rep", "tile"), None, None), P(), P(), P(), P())
    return jax.shard_map(body, mesh=mesh, in_specs=in_specs, out_specs=out_specs, check_vma=False)
```

```python
import jax
import jax.numpy as jnp
from jax import lax
from jax.sharding import PartitionSpec as P

IMG_DEV = 2
H = 48
W = 72
RATE = 12


def padded(x, sides, width):
    for axis, dim in sides:
        size, length = (lax.axis_size(axis), x.shape[dim])
        up = [(i, (i + 1) % size) for i in range(size - 1)]
        down = [(j, i) for i, j in up]
        last = lax.slice_in_dim(x, length - width, length, axis=dim)
        first = lax.slice_in_dim(x, 0, width, axis=dim)
        before = lax.ppermute(last, axis, up)
        after = lax.ppermute(first, axis, down)
        x = jnp.concatenate([before, x, after], axis=dim)
    return x


def index_bits(axes):
    bits = []
    for axis in reversed(axes):
        size = lax.axis_size(axis)
        assert size & (size - 1) == 0
        bits += [(axis, b) for b in range(size.bit_length() - 1)]
    return bits


def exchange(x, axis, bit):
    size = lax.axis_size(axis)
    pairs = [(i, i ^ (1 << bit)) for i in range(size)]
    return lax.ppermute(x, axis, pairs)


def butterfly_sum(x, axes):
    for axis, bit in index_bits(axes):
        x = jax.tree.map(lambda v, w: v + w, x, exchange(x, axis, bit))
    return x


def halving_scatter(x, steps, bit_axes):
    bit_axes = list(bit_axes)
    for axis, bit, combined in steps:
        ax = bit_axes.index(combined)
        mine = (lax.axis_index(axis) >> bit) & 1
        keep = lax.dynamic_index_in_dim(x, mine, ax, keepdims=False)
        send = lax.dynamic_index_in_dim(x, 1 - mine, ax, keepdims=False)
        x = keep + exchange(send, axis, bit)
        bit_axes.pop(ax)
    return x


def body(
    features,
    conv_out,
    conv_weight,
    norm_gain_vector,
    norm_shift_vector,
    class_map,
    labels,
    class_weight,
):
    highest = lax.Precision.HIGHEST
    images, tile_rows, columns, in_chans = features.shape
    out_chans = conv_out.shape[3]
    taps = conv_weight.shape[0]
    local_pix = images * tile_rows * columns
    per_replica_part = IMG_DEV * H * W
    all_pix = lax.axis_size("rep") * per_replica_part
    classes = class_map.shape[0]

    onehot = (
        labels.reshape(local_pix, 1) == jnp.arange(classes, dtype=jnp.int32)
    ).astype(jnp.float32)
    weights_pix = jnp.sum(onehot * class_weight.astype(jnp.float32), -1)

    yvals = conv_out.astype(jnp.float32).reshape(local_pix, out_chans)
    tiles = lax.axis_size("tile")
    local_sum = jnp.sum(yvals, 0)
    local_offset = yvals - local_sum / local_pix
    local_stats = jnp.concatenate(
        [local_sum, jnp.sum(local_offset * local_offset, 0), jnp.sum(weights_pix)[None]]
    )
    slot = (jnp.arange(tiles) == lax.axis_index("tile")).astype(jnp.float32)
    tile_stats = lax.psum(slot[:, None] * local_stats[None, :], "tile")
    tile_sums = tile_stats[:, :out_chans]
    column_sum = jnp.sum(tile_sums, 0)
    tile_means = tile_sums / local_pix - column_sum / per_replica_part
    variance = (
        jnp.sum(tile_stats[:, out_chans : 2 * out_chans] + local_pix * tile_means * tile_means, 0)
        / per_replica_part
    )
    weight_total = butterfly_sum(jnp.sum(tile_stats[:, 2 * out_chans]), ("rep",))
    centre_offset = yvals - column_sum / per_replica_part
    inverse_deviation = lax.rsqrt(variance + 1e-05)
    normalized_input = centre_offset * inverse_deviation
    preactivation_values = norm_gain_vector * normalized_input + norm_shift_vector
    zvals = jnp.maximum(preactivation_values, 0.0)
    logits = jnp.dot(zvals, class_map.T, precision=highest)
    top_val = jnp.max(logits, -1, keepdims=True)
    log_total = top_val[:, 0] + jnp.log(jnp.sum(jnp.exp(logits - top_val), -1))
    cross = log_total - jnp.sum(onehot * logits, -1)
    mean_weight = weight_total / all_pix
    probs = jnp.exp(logits - log_total[:, None])
    grad_logit = weights_pix[:, None] * (probs - onehot)
    class_local_slice = jnp.dot(grad_logit.T, zvals, precision=highest)
    grad_z = jnp.dot(grad_logit, class_map, precision=highest)
    preactivation_gradient = jnp.where(preactivation_values > 0, grad_z, 0.0)
    first_gradient_sum, second_gradient_sum, class_tile, loss_tile = lax.psum(
        (
            jnp.sum(preactivation_gradient, 0),
            jnp.sum(preactivation_gradient * normalized_input, 0),
            class_local_slice,
            jnp.sum(weights_pix * cross),
        ),
        "tile",
    )
    packed = jnp.concatenate(
        [first_gradient_sum, second_gradient_sum, class_tile.reshape(-1), loss_tile[None]]
    )
    normalized_output_gradient = (
        norm_gain_vector
        * inverse_deviation
        * (
            (
                preactivation_gradient
                - first_gradient_sum / per_replica_part
                - normalized_input * second_gradient_sum / per_replica_part
            )
            / mean_weight
        )
    ).astype(jnp.bfloat16)
    normalized_output_gradient = normalized_output_gradient.reshape(
        images, tile_rows, columns, out_chans
    )
    column_pad = ((0, 0), (0, 0), (RATE, RATE), (0, 0))
    extended = jnp.pad(padded(normalized_output_gradient, (("tile", 1),), RATE), column_pad)
    own_rows = jnp.pad(normalized_output_gradient, column_pad)
    shifted_list = []
    for tap_index in range(taps):
        row_off = RATE - (tap_index // 3 - 1) * RATE
        col_off = RATE - (tap_index % 3 - 1) * RATE
        if tap_index // 3 == 1:
            piece = own_rows[:, :, col_off : col_off + columns, :]
        else:
            piece = extended[:, row_off : row_off + tile_rows, col_off : col_off + columns, :]
        shifted_list.append(piece.reshape(local_pix, out_chans))
    shifted = jnp.concatenate(shifted_list, 1)

    blocks = lax.axis_size("rep") * lax.axis_size("tile")
    nbits = blocks.bit_length() - 1
    rows = in_chans // blocks
    flat_x = features.reshape(local_pix, in_chans)
    packed, flat_x = lax.optimization_barrier((packed, flat_x))
    bits = [(axis, bit, combined) for combined, (axis, bit) in enumerate(index_bits(("rep", "tile")))]
    rest = bits[1:]
    orders = [rest, rest[1:] + rest[:1], rest[2:3] + rest[:2] + rest[3:]]
    group_taps = [taps - 2 * (taps // 3), taps // 3, taps // 3]
    starts = [sum(group_taps[:s]) for s in range(3)]
    parts = []
    for s in range(3):
        cols = jnp.concatenate(shifted_list[starts[s] : starts[s] + group_taps[s]], 1)
        part = lax.dot_general(
            flat_x, cols, (((0,), (0,)), ((), ())), preferred_element_type=jnp.float32
        )
        parts.append(part.reshape((2,) * nbits + (rows, group_taps[s] * out_chans)))

    halves = 2
    share = in_chans // halves
    grad_chunks = [
        lax.dot_general(
            shifted.reshape(local_pix, taps, out_chans),
            conv_weight[:, h * share : (h + 1) * share, :],
            (((1, 2), (0, 2)), ((), ())),
            preferred_element_type=jnp.float32,
        ).astype(jnp.bfloat16)
        for h in range(halves)
    ]
    axis, bit, combined = bits[0]
    bit_axes = list(range(nbits - 1, -1, -1))
    ax = bit_axes.index(combined)
    mine = (lax.axis_index(axis) >> bit) & 1
    keeps = [lax.dynamic_index_in_dim(p, mine, ax, keepdims=False) for p in parts]
    sends = [lax.dynamic_index_in_dim(p, 1 - mine, ax, keepdims=False) for p in parts]
    received = lax.optimization_barrier([exchange(v, axis, bit) for v in sends])
    bit_axes.pop(ax)
    pieces = [keeps[s] + received[s] for s in range(3)]
    small_bits = index_bits(("rep",))
    axes_of = [list(bit_axes) for s in range(3)]
    for step in range(len(rest)):
        sends, keeps = [], []
        for s in range(3):
            axis, bit, combined = orders[s][step]
            ax = axes_of[s].index(combined)
            mine = (lax.axis_index(axis) >> bit) & 1
            keeps.append(lax.dynamic_index_in_dim(pieces[s], mine, ax, keepdims=False))
            sends.append(lax.dynamic_index_in_dim(pieces[s], 1 - mine, ax, keepdims=False))
            axes_of[s].pop(ax)
        received = []
        if step < len(small_bits):
            packed, sends = lax.optimization_barrier((packed, sends))
            received.append(exchange(packed, *small_bits[step]))
        received = [exchange(sends[s], orders[s][step][0], orders[s][step][1]) for s in range(3)] + received
        if step < halves:
            received, grad_chunks[step] = lax.optimization_barrier((received, grad_chunks[step]))
        else:
            received = lax.optimization_barrier(received)
        if step < len(small_bits):
            packed = packed + received.pop()
        pieces = [keeps[s] + received[s] for s in range(3)]
    grad_weight = jnp.concatenate(pieces, 1).reshape(rows, taps, out_chans)

    for step in range(len(rest), len(small_bits)):
        packed = packed + exchange(packed, *small_bits[step])
    grad_shift = packed[:out_chans] / mean_weight
    grad_gain = packed[out_chans : 2 * out_chans] / mean_weight
    grad_class = packed[2 * out_chans : (2 + classes) * out_chans].reshape(classes, out_chans) / mean_weight
    loss = packed[(2 + classes) * out_chans] / mean_weight / all_pix
    grad_features = jnp.concatenate(grad_chunks, 1).reshape(images, tile_rows, columns, in_chans)
    return (grad_features, grad_weight, grad_gain, grad_shift, grad_class, loss)


def solution(mesh):
    in_specs = (
        P("rep", "tile", None, None),
        P("rep", "tile", None, None),
        P(),
        P(),
        P(),
        P(),
        P("rep", "tile", None),
        P(),
    )
    out_specs = (P("rep", "tile", None, None), P(("rep", "tile"), None, None), P(), P(), P(), P())
    return jax.shard_map(body, mesh=mesh, in_specs=in_specs, out_specs=out_specs, check_vma=False)
```

```python
import jax
import jax.numpy as jnp
from jax import lax
from jax.sharding import PartitionSpec as P

IMG_DEV = 2
H = 48
W = 72
RATE = 12


def padded(x, sides, width):
    for axis, dim in sides:
        size, length = (lax.axis_size(axis), x.shape[dim])
        up = [(i, (i + 1) % size) for i in range(size - 1)]
        down = [(j, i) for i, j in up]
        last = lax.slice_in_dim(x, length - width, length, axis=dim)
        first = lax.slice_in_dim(x, 0, width, axis=dim)
        before = lax.ppermute(last, axis, up)
        after = lax.ppermute(first, axis, down)
        x = jnp.concatenate([before, x, after], axis=dim)
    return x


def index_bits(axes):
    bits = []
    for axis in reversed(axes):
        size = lax.axis_size(axis)
        assert size & (size - 1) == 0
        bits += [(axis, b) for b in range(size.bit_length() - 1)]
    return bits


def exchange(x, axis, bit):
    size = lax.axis_size(axis)
    pairs = [(i, i ^ (1 << bit)) for i in range(size)]
    return lax.ppermute(x, axis, pairs)


def butterfly_sum(x, axes):
    steps = [a for a in axes if isinstance(a, tuple)] or index_bits(axes)
    for axis, bit in steps:
        x = jax.tree.map(lambda v, w: v + w, x, exchange(x, axis, bit))
    return x


def halving_scatter(x, steps, bit_axes):
    bit_axes = list(bit_axes)
    for axis, bit, combined in steps:
        ax = bit_axes.index(combined)
        mine = (lax.axis_index(axis) >> bit) & 1
        keep = lax.dynamic_index_in_dim(x, mine, ax, keepdims=False)
        send = lax.dynamic_index_in_dim(x, 1 - mine, ax, keepdims=False)
        x = keep + exchange(send, axis, bit)
        bit_axes.pop(ax)
    return x


def body(
    features,
    conv_out,
    conv_weight,
    norm_gain_vector,
    norm_shift_vector,
    class_map,
    labels,
    class_weight,
):
    highest = lax.Precision.HIGHEST
    images, tile_rows, columns, in_chans = features.shape
    out_chans = conv_out.shape[3]
    taps = conv_weight.shape[0]
    local_pix = images * tile_rows * columns
    per_replica_part = IMG_DEV * H * W
    all_pix = lax.axis_size("rep") * per_replica_part
    classes = class_map.shape[0]

    onehot = (
        labels.reshape(local_pix, 1) == jnp.arange(classes, dtype=jnp.int32)
    ).astype(jnp.float32)
    weights_pix = jnp.sum(onehot * class_weight.astype(jnp.float32), -1)

    yvals = conv_out.astype(jnp.float32).reshape(local_pix, out_chans)
    tiles = lax.axis_size("tile")
    local_sum = jnp.sum(yvals, 0)
    local_offset = yvals - local_sum / local_pix
    local_stats = jnp.concatenate(
        [local_sum, jnp.sum(local_offset * local_offset, 0), jnp.sum(weights_pix)[None]]
    )
    slot = (jnp.arange(tiles) == lax.axis_index("tile")).astype(jnp.float32)
    tile_stats = lax.psum(slot[:, None] * local_stats[None, :], "tile")
    tile_sums = tile_stats[:, :out_chans]
    column_sum = jnp.sum(tile_sums, 0)
    tile_means = tile_sums / local_pix - column_sum / per_replica_part
    variance = (
        jnp.sum(tile_stats[:, out_chans : 2 * out_chans] + local_pix * tile_means * tile_means, 0)
        / per_replica_part
    )
    weight_pair = butterfly_sum(jnp.sum(tile_stats[:, 2 * out_chans]), (("rep", 0),))
    reps = lax.axis_size("rep")
    weight_total = weight_pair
    for k in range(1, reps // 2):
        pairs = [(i, i ^ (k << 1)) for i in range(reps)]
        weight_total = weight_total + lax.ppermute(weight_pair, "rep", pairs)
    centre_offset = yvals - column_sum / per_replica_part
    inverse_deviation = lax.rsqrt(variance + 1e-05)
    normalized_input = centre_offset * inverse_deviation
    preactivation_values = norm_gain_vector * normalized_input + norm_shift_vector
    zvals = jnp.maximum(preactivation_values, 0.0)
    logits = jnp.dot(zvals, class_map.T, precision=highest)
    top_val = jnp.max(logits, -1, keepdims=True)
    log_total = top_val[:, 0] + jnp.log(jnp.sum(jnp.exp(logits - top_val), -1))
    cross = log_total - jnp.sum(onehot * logits, -1)
    mean_weight = weight_total / all_pix
    probs = jnp.exp(logits - log_total[:, None])
    grad_logit = weights_pix[:, None] * (probs - onehot)
    class_local_slice = jnp.dot(grad_logit.T, zvals, precision=highest)
    grad_z = jnp.dot(grad_logit, class_map, precision=highest)
    preactivation_gradient = jnp.where(preactivation_values > 0, grad_z, 0.0)
    first_gradient_sum, second_gradient_sum, class_tile, loss_tile = lax.psum(
        (
            jnp.sum(preactivation_gradient, 0),
            jnp.sum(preactivation_gradient * normalized_input, 0),
            class_local_slice,
            jnp.sum(weights_pix * cross),
        ),
        "tile",
    )
    packed = jnp.concatenate(
        [first_gradient_sum, second_gradient_sum, class_tile.reshape(-1), loss_tile[None]]
    )
    normalized_output_gradient = (
        norm_gain_vector
        * inverse_deviation
        * (
            (
                preactivation_gradient
                - first_gradient_sum / per_replica_part
                - normalized_input * second_gradient_sum / per_replica_part
            )
            / mean_weight
        )
    ).astype(jnp.bfloat16)
    normalized_output_gradient = normalized_output_gradient.reshape(
        images, tile_rows, columns, out_chans
    )
    column_pad = ((0, 0), (0, 0), (RATE, RATE), (0, 0))
    extended = jnp.pad(padded(normalized_output_gradient, (("tile", 1),), RATE), column_pad)
    own_rows = jnp.pad(normalized_output_gradient, column_pad)
    shifted_list = []
    for tap_index in range(taps):
        row_off = RATE - (tap_index // 3 - 1) * RATE
        col_off = RATE - (tap_index % 3 - 1) * RATE
        if tap_index // 3 == 1:
            piece = own_rows[:, :, col_off : col_off + columns, :]
        else:
            piece = extended[:, row_off : row_off + tile_rows, col_off : col_off + columns, :]
        shifted_list.append(piece.reshape(local_pix, out_chans))
    shifted = jnp.concatenate(shifted_list, 1)

    blocks = lax.axis_size("rep") * lax.axis_size("tile")
    nbits = blocks.bit_length() - 1
    rows = in_chans // blocks
    flat_x = features.reshape(local_pix, in_chans)
    packed, flat_x = lax.optimization_barrier((packed, flat_x))
    bits = [(axis, bit, combined) for combined, (axis, bit) in enumerate(index_bits(("rep", "tile")))]
    rest = bits[1:]
    orders = [rest, rest[1:] + rest[:1], rest[2:3] + rest[:2] + rest[3:]]
    group_taps = [taps - 2 * (taps // 3), taps // 3, taps // 3]
    starts = [sum(group_taps[:s]) for s in range(3)]
    parts = []
    for s in range(3):
        cols = jnp.concatenate(shifted_list[starts[s] : starts[s] + group_taps[s]], 1)
        part = lax.dot_general(
            flat_x, cols, (((0,), (0,)), ((), ())), preferred_element_type=jnp.float32
        )
        parts.append(part.reshape((2,) * nbits + (rows, group_taps[s] * out_chans)))

    halves = 2
    share = in_chans // halves
    grad_chunks = [
        lax.dot_general(
            shifted.reshape(local_pix, taps, out_chans),
            conv_weight[:, h * share : (h + 1) * share, :],
            (((1, 2), (0, 2)), ((), ())),
            preferred_element_type=jnp.float32,
        ).astype(jnp.bfloat16)
        for h in range(halves)
    ]
    axis, bit, combined = bits[0]
    bit_axes = list(range(nbits - 1, -1, -1))
    ax = bit_axes.index(combined)
    mine = (lax.axis_index(axis) >> bit) & 1
    keeps = [lax.dynamic_index_in_dim(p, mine, ax, keepdims=False) for p in parts]
    sends = [lax.dynamic_index_in_dim(p, 1 - mine, ax, keepdims=False) for p in parts]
    received = lax.optimization_barrier([exchange(v, axis, bit) for v in sends])
    bit_axes.pop(ax)
    pieces = [keeps[s] + received[s] for s in range(3)]
    small_bits = index_bits(("rep",))
    axes_of = [list(bit_axes) for s in range(3)]
    for step in range(len(rest)):
        sends, keeps = [], []
        for s in range(3):
            axis, bit, combined = orders[s][step]
            ax = axes_of[s].index(combined)
            mine = (lax.axis_index(axis) >> bit) & 1
            keeps.append(lax.dynamic_index_in_dim(pieces[s], mine, ax, keepdims=False))
            sends.append(lax.dynamic_index_in_dim(pieces[s], 1 - mine, ax, keepdims=False))
            axes_of[s].pop(ax)
        received = []
        if step < len(small_bits):
            packed, sends = lax.optimization_barrier((packed, sends))
            received.append(exchange(packed, *small_bits[step]))
        received = [exchange(sends[s], orders[s][step][0], orders[s][step][1]) for s in range(3)] + received
        if step < halves:
            received, grad_chunks[step] = lax.optimization_barrier((received, grad_chunks[step]))
        else:
            received = lax.optimization_barrier(received)
        if step < len(small_bits):
            packed = packed + received.pop()
        pieces = [keeps[s] + received[s] for s in range(3)]
    grad_weight = jnp.concatenate(pieces, 1).reshape(rows, taps, out_chans)

    for step in range(len(rest), len(small_bits)):
        packed = packed + exchange(packed, *small_bits[step])
    grad_shift = packed[:out_chans] / mean_weight
    grad_gain = packed[out_chans : 2 * out_chans] / mean_weight
    grad_class = packed[2 * out_chans : (2 + classes) * out_chans].reshape(classes, out_chans) / mean_weight
    loss = packed[(2 + classes) * out_chans] / mean_weight / all_pix
    grad_features = jnp.concatenate(grad_chunks, 1).reshape(images, tile_rows, columns, in_chans)
    return (grad_features, grad_weight, grad_gain, grad_shift, grad_class, loss)


def solution(mesh):
    in_specs = (
        P("rep", "tile", None, None),
        P("rep", "tile", None, None),
        P(),
        P(),
        P(),
        P(),
        P("rep", "tile", None),
        P(),
    )
    out_specs = (P("rep", "tile", None, None), P(("rep", "tile"), None, None), P(), P(), P(), P())
    return jax.shard_map(body, mesh=mesh, in_specs=in_specs, out_specs=out_specs, check_vma=False)
```

```python
import jax
import jax.numpy as jnp
from jax import lax
from jax.sharding import PartitionSpec as P

IMG_DEV = 2
H = 48
W = 72
RATE = 12


def padded(x, sides, width):
    for axis, dim in sides:
        size, length = (lax.axis_size(axis), x.shape[dim])
        up = [(i, (i + 1) % size) for i in range(size - 1)]
        down = [(j, i) for i, j in up]
        last = lax.slice_in_dim(x, length - width, length, axis=dim)
        first = lax.slice_in_dim(x, 0, width, axis=dim)
        before = lax.ppermute(last, axis, up)
        after = lax.ppermute(first, axis, down)
        x = jnp.concatenate([before, x, after], axis=dim)
    return x


def index_bits(axes):
    bits = []
    for axis in reversed(axes):
        size = lax.axis_size(axis)
        assert size & (size - 1) == 0
        bits += [(axis, b) for b in range(size.bit_length() - 1)]
    return bits


def exchange(x, axis, bit):
    size = lax.axis_size(axis)
    pairs = [(i, i ^ (1 << bit)) for i in range(size)]
    return lax.ppermute(x, axis, pairs)


def butterfly_sum(x, axes):
    for axis, bit in index_bits(axes):
        x = jax.tree.map(lambda v, w: v + w, x, exchange(x, axis, bit))
    return x


def halving_scatter(x, steps, bit_axes):
    bit_axes = list(bit_axes)
    for axis, bit, combined in steps:
        ax = bit_axes.index(combined)
        mine = (lax.axis_index(axis) >> bit) & 1
        keep = lax.dynamic_index_in_dim(x, mine, ax, keepdims=False)
        send = lax.dynamic_index_in_dim(x, 1 - mine, ax, keepdims=False)
        x = keep + exchange(send, axis, bit)
        bit_axes.pop(ax)
    return x


def body(
    features,
    conv_out,
    conv_weight,
    norm_gain_vector,
    norm_shift_vector,
    class_map,
    labels,
    class_weight,
):
    highest = lax.Precision.HIGHEST
    images, tile_rows, columns, in_chans = features.shape
    out_chans = conv_out.shape[3]
    taps = conv_weight.shape[0]
    local_pix = images * tile_rows * columns
    per_replica_part = IMG_DEV * H * W
    all_pix = lax.axis_size("rep") * per_replica_part
    classes = class_map.shape[0]

    onehot = (
        labels.reshape(local_pix, 1) == jnp.arange(classes, dtype=jnp.int32)
    ).astype(jnp.float32)
    weights_pix = jnp.sum(onehot * class_weight.astype(jnp.float32), -1)

    yvals = conv_out.astype(jnp.float32).reshape(local_pix, out_chans)
    tiles = lax.axis_size("tile")
    local_sum = jnp.sum(yvals, 0)
    local_offset = yvals - local_sum / local_pix
    local_stats = jnp.concatenate(
        [local_sum, jnp.sum(local_offset * local_offset, 0), jnp.sum(weights_pix)[None]]
    )
    slot = (jnp.arange(tiles) == lax.axis_index("tile")).astype(jnp.float32)
    tile_stats = lax.psum(slot[:, None] * local_stats[None, :], "tile")
    tile_sums = tile_stats[:, :out_chans]
    column_sum = jnp.sum(tile_sums, 0)
    tile_means = tile_sums / local_pix - column_sum / per_replica_part
    variance = (
        jnp.sum(tile_stats[:, out_chans : 2 * out_chans] + local_pix * tile_means * tile_means, 0)
        / per_replica_part
    )
    weight_total = butterfly_sum(jnp.sum(tile_stats[:, 2 * out_chans]), ("rep",))
    centre_offset = yvals - column_sum / per_replica_part
    inverse_deviation = lax.rsqrt(variance + 1e-05)
    normalized_input = centre_offset * inverse_deviation
    preactivation_values = norm_gain_vector * normalized_input + norm_shift_vector
    zvals = jnp.maximum(preactivation_values, 0.0)
    logits = jnp.dot(zvals, class_map.T, precision=highest)
    top_val = jnp.max(logits, -1, keepdims=True)
    log_total = top_val[:, 0] + jnp.log(jnp.sum(jnp.exp(logits - top_val), -1))
    cross = log_total - jnp.sum(onehot * logits, -1)
    mean_weight = weight_total / all_pix
    probs = jnp.exp(logits - log_total[:, None])
    grad_logit = weights_pix[:, None] * (probs - onehot)
    class_local_slice = jnp.dot(grad_logit.T, zvals, precision=highest)
    grad_z = jnp.dot(grad_logit, class_map, precision=highest)
    preactivation_gradient = jnp.where(preactivation_values > 0, grad_z, 0.0)
    first_gradient_sum, second_gradient_sum, class_tile, loss_tile = lax.psum(
        (
            jnp.sum(preactivation_gradient, 0),
            jnp.sum(preactivation_gradient * normalized_input, 0),
            class_local_slice,
            jnp.sum(weights_pix * cross),
        ),
        "tile",
    )
    packed = jnp.concatenate(
        [first_gradient_sum, second_gradient_sum, class_tile.reshape(-1), loss_tile[None]]
    )
    normalized_output_gradient = (
        norm_gain_vector
        * inverse_deviation
        * (
            (
                preactivation_gradient
                - first_gradient_sum / per_replica_part
                - normalized_input * second_gradient_sum / per_replica_part
            )
            / mean_weight
        )
    ).astype(jnp.bfloat16)
    normalized_output_gradient = normalized_output_gradient.reshape(
        images, tile_rows, columns, out_chans
    )
    column_pad = ((0, 0), (0, 0), (RATE, RATE), (0, 0))
    extended = jnp.pad(padded(normalized_output_gradient, (("tile", 1),), RATE), column_pad)
    own_rows = jnp.pad(normalized_output_gradient, column_pad)
    shifted_list = []
    for tap_index in range(taps):
        row_off = RATE - (tap_index // 3 - 1) * RATE
        col_off = RATE - (tap_index % 3 - 1) * RATE
        if tap_index // 3 == 1:
            piece = own_rows[:, :, col_off : col_off + columns, :]
        else:
            piece = extended[:, row_off : row_off + tile_rows, col_off : col_off + columns, :]
        shifted_list.append(piece.reshape(local_pix, out_chans))
    shifted = jnp.concatenate(shifted_list, 1)

    blocks = lax.axis_size("rep") * lax.axis_size("tile")
    nbits = blocks.bit_length() - 1
    rows = in_chans // blocks
    flat_x = features.reshape(local_pix, in_chans)
    packed, flat_x = lax.optimization_barrier((packed, flat_x))
    bits = [(axis, bit, combined) for combined, (axis, bit) in enumerate(index_bits(("rep", "tile")))]
    rest = bits[1:]
    orders = [rest, rest[1:] + rest[:1], rest[2:3] + rest[:2] + rest[3:]]
    group_taps = [taps - 2 * (taps // 3), taps // 3, taps // 3]
    starts = [sum(group_taps[:s]) for s in range(3)]
    parts = []
    for s in range(3):
        cols = jnp.concatenate(shifted_list[starts[s] : starts[s] + group_taps[s]], 1)
        part = lax.dot_general(
            flat_x, cols, (((0,), (0,)), ((), ())), preferred_element_type=jnp.float32
        )
        parts.append(part.reshape((2,) * nbits + (rows, group_taps[s] * out_chans)))

    halves = 2
    share = in_chans // halves
    grad_chunks = [
        lax.dot_general(
            shifted.reshape(local_pix, taps, out_chans),
            conv_weight[:, h * share : (h + 1) * share, :],
            (((1, 2), (0, 2)), ((), ())),
            preferred_element_type=jnp.float32,
        ).astype(jnp.bfloat16)
        for h in range(halves)
    ]
    axis, bit, combined = bits[0]
    bit_axes = list(range(nbits - 1, -1, -1))
    ax = bit_axes.index(combined)
    mine = (lax.axis_index(axis) >> bit) & 1
    keeps = [lax.dynamic_index_in_dim(p, mine, ax, keepdims=False) for p in parts]
    sends = [lax.dynamic_index_in_dim(p, 1 - mine, ax, keepdims=False) for p in parts]
    received = lax.optimization_barrier([exchange(v, axis, bit) for v in sends])
    bit_axes.pop(ax)
    pieces = [(keeps[s], received[s]) for s in range(3)]
    small_bits = index_bits(("rep",))
    axes_of = [list(bit_axes) for s in range(3)]
    for step in range(len(rest)):
        sends, keeps = [], []
        for s in range(3):
            axis, bit, combined = orders[s][step]
            ax = axes_of[s].index(combined)
            mine = (lax.axis_index(axis) >> bit) & 1
            own, other = pieces[s]
            keeps.append(
                lax.dynamic_index_in_dim(own, mine, ax, keepdims=False)
                + lax.dynamic_index_in_dim(other, mine, ax, keepdims=False)
            )
            sends.append(
                lax.dynamic_index_in_dim(own, 1 - mine, ax, keepdims=False)
                + lax.dynamic_index_in_dim(other, 1 - mine, ax, keepdims=False)
            )
            axes_of[s].pop(ax)
        received = []
        if step < len(small_bits):
            packed, sends = lax.optimization_barrier((packed, sends))
            received.append(exchange(packed, *small_bits[step]))
        received = [exchange(sends[s], orders[s][step][0], orders[s][step][1]) for s in range(3)] + received
        if step < halves:
            received, grad_chunks[step] = lax.optimization_barrier((received, grad_chunks[step]))
        else:
            received = lax.optimization_barrier(received)
        if step < len(small_bits):
            packed = packed + received.pop()
        pieces = [(keeps[s], received[s]) for s in range(3)]
    grad_weight = jnp.concatenate([own + other for own, other in pieces], 1).reshape(rows, taps, out_chans)

    for step in range(len(rest), len(small_bits)):
        packed = packed + exchange(packed, *small_bits[step])
    grad_shift = packed[:out_chans] / mean_weight
    grad_gain = packed[out_chans : 2 * out_chans] / mean_weight
    grad_class = packed[2 * out_chans : (2 + classes) * out_chans].reshape(classes, out_chans) / mean_weight
    loss = packed[(2 + classes) * out_chans] / mean_weight / all_pix
    grad_features = jnp.concatenate(grad_chunks, 1).reshape(images, tile_rows, columns, in_chans)
    return (grad_features, grad_weight, grad_gain, grad_shift, grad_class, loss)


def solution(mesh):
    in_specs = (
        P("rep", "tile", None, None),
        P("rep", "tile", None, None),
        P(),
        P(),
        P(),
        P(),
        P("rep", "tile", None),
        P(),
    )
    out_specs = (P("rep", "tile", None, None), P(("rep", "tile"), None, None), P(), P(), P(), P())
    return jax.shard_map(body, mesh=mesh, in_specs=in_specs, out_specs=out_specs, check_vma=False)
```

```python
import jax
import jax.numpy as jnp
from jax import lax
from jax.sharding import PartitionSpec as P

IMG_DEV = 2
H = 48
W = 72
RATE = 12


def padded(x, sides, width):
    for axis, dim in sides:
        size, length = (lax.axis_size(axis), x.shape[dim])
        up = [(i, (i + 1) % size) for i in range(size - 1)]
        down = [(j, i) for i, j in up]
        last = lax.slice_in_dim(x, length - width, length, axis=dim)
        first = lax.slice_in_dim(x, 0, width, axis=dim)
        before = lax.ppermute(last, axis, up)
        after = lax.ppermute(first, axis, down)
        x = jnp.concatenate([before, x, after], axis=dim)
    return x


def index_bits(axes):
    bits = []
    for axis in reversed(axes):
        size = lax.axis_size(axis)
        assert size & (size - 1) == 0
        bits += [(axis, b) for b in range(size.bit_length() - 1)]
    return bits


def exchange(x, axis, bit):
    size = lax.axis_size(axis)
    pairs = [(i, i ^ (1 << bit)) for i in range(size)]
    return lax.ppermute(x, axis, pairs)


def butterfly_sum(x, axes):
    for axis, bit in index_bits(axes):
        x = jax.tree.map(lambda v, w: v + w, x, exchange(x, axis, bit))
    return x


def halving_scatter(x, steps, bit_axes):
    bit_axes = list(bit_axes)
    for axis, bit, combined in steps:
        ax = bit_axes.index(combined)
        mine = (lax.axis_index(axis) >> bit) & 1
        keep = lax.dynamic_index_in_dim(x, mine, ax, keepdims=False)
        send = lax.dynamic_index_in_dim(x, 1 - mine, ax, keepdims=False)
        x = keep + exchange(send, axis, bit)
        bit_axes.pop(ax)
    return x


def body(
    features,
    conv_out,
    conv_weight,
    norm_gain_vector,
    norm_shift_vector,
    class_map,
    labels,
    class_weight,
):
    highest = lax.Precision.HIGHEST
    images, tile_rows, columns, in_chans = features.shape
    out_chans = conv_out.shape[3]
    taps = conv_weight.shape[0]
    local_pix = images * tile_rows * columns
    per_replica_part = IMG_DEV * H * W
    all_pix = lax.axis_size("rep") * per_replica_part
    classes = class_map.shape[0]

    onehot = (
        labels.reshape(local_pix, 1) == jnp.arange(classes, dtype=jnp.int32)
    ).astype(jnp.float32)
    weights_pix = jnp.sum(onehot * class_weight.astype(jnp.float32), -1)

    yvals = conv_out.astype(jnp.float32).reshape(local_pix, out_chans)
    tiles = lax.axis_size("tile")
    local_sum = jnp.sum(yvals, 0)
    local_offset = yvals - local_sum / local_pix
    local_stats = jnp.concatenate(
        [local_sum, jnp.sum(local_offset * local_offset, 0), jnp.sum(weights_pix)[None]]
    )
    slot = (jnp.arange(tiles) == lax.axis_index("tile")).astype(jnp.float32)
    tile_stats = lax.psum(slot[:, None] * local_stats[None, :], "tile")
    tile_sums = tile_stats[:, :out_chans]
    column_sum = jnp.sum(tile_sums, 0)
    tile_means = tile_sums / local_pix - column_sum / per_replica_part
    variance = (
        jnp.sum(tile_stats[:, out_chans : 2 * out_chans] + local_pix * tile_means * tile_means, 0)
        / per_replica_part
    )
    weight_total = butterfly_sum(jnp.sum(tile_stats[:, 2 * out_chans]), ("rep",))
    centre_offset = yvals - column_sum / per_replica_part
    inverse_deviation = lax.rsqrt(variance + 1e-05)
    normalized_input = centre_offset * inverse_deviation
    preactivation_values = norm_gain_vector * normalized_input + norm_shift_vector
    zvals = jnp.maximum(preactivation_values, 0.0)
    logits = jnp.dot(zvals, class_map.T, precision=highest)
    top_val = jnp.max(logits, -1, keepdims=True)
    log_total = top_val[:, 0] + jnp.log(jnp.sum(jnp.exp(logits - top_val), -1))
    cross = log_total - jnp.sum(onehot * logits, -1)
    mean_weight = weight_total / all_pix
    probs = jnp.exp(logits - log_total[:, None])
    grad_logit = weights_pix[:, None] * (probs - onehot)
    class_local_slice = jnp.dot(grad_logit.T, zvals, precision=highest)
    grad_z = jnp.dot(grad_logit, class_map, precision=highest)
    preactivation_gradient = jnp.where(preactivation_values > 0, grad_z, 0.0)
    first_gradient_sum, second_gradient_sum, class_tile, loss_tile = lax.psum(
        (
            jnp.sum(preactivation_gradient, 0),
            jnp.sum(preactivation_gradient * normalized_input, 0),
            class_local_slice,
            jnp.sum(weights_pix * cross),
        ),
        "tile",
    )
    packed = jnp.concatenate(
        [first_gradient_sum, second_gradient_sum, class_tile.reshape(-1), loss_tile[None]]
    )
    normalized_output_gradient = (
        norm_gain_vector
        * inverse_deviation
        * (
            (
                preactivation_gradient
                - first_gradient_sum / per_replica_part
                - normalized_input * second_gradient_sum / per_replica_part
            )
            / mean_weight
        )
    ).astype(jnp.bfloat16)
    normalized_output_gradient = normalized_output_gradient.reshape(
        images, tile_rows, columns, out_chans
    )
    column_pad = ((0, 0), (0, 0), (RATE, RATE), (0, 0))
    extended = jnp.pad(padded(normalized_output_gradient, (("tile", 1),), RATE), column_pad)
    own_rows = jnp.pad(normalized_output_gradient, column_pad)
    shifted_list = []
    for tap_index in range(taps):
        row_off = RATE - (tap_index // 3 - 1) * RATE
        col_off = RATE - (tap_index % 3 - 1) * RATE
        if tap_index // 3 == 1:
            piece = own_rows[:, :, col_off : col_off + columns, :]
        else:
            piece = extended[:, row_off : row_off + tile_rows, col_off : col_off + columns, :]
        shifted_list.append(piece.reshape(local_pix, out_chans))
    shifted = jnp.concatenate(shifted_list, 1)

    blocks = lax.axis_size("rep") * lax.axis_size("tile")
    nbits = blocks.bit_length() - 1
    rows = in_chans // blocks
    flat_x = features.reshape(local_pix, in_chans)
    packed, flat_x = lax.optimization_barrier((packed, flat_x))
    bits = [(axis, bit, combined) for combined, (axis, bit) in enumerate(index_bits(("rep", "tile")))]
    rest = bits[1:]
    orders = [rest, rest[1:] + rest[:1], rest[2:3] + rest[:2] + rest[3:]]
    group_taps = [taps - 2 * (taps // 3), taps // 3, taps // 3]
    starts = [sum(group_taps[:s]) for s in range(3)]
    parts = []
    for s in range(3):
        cols = jnp.concatenate(shifted_list[starts[s] : starts[s] + group_taps[s]], 1)
        part = lax.dot_general(
            flat_x, cols, (((0,), (0,)), ((), ())), preferred_element_type=jnp.float32
        )
        parts.append(part.reshape((2,) * nbits + (rows, group_taps[s] * out_chans)))

    halves = 2
    share = in_chans // halves
    grad_chunks = [
        lax.dot_general(
            shifted.reshape(local_pix, taps, out_chans),
            conv_weight[:, h * share : (h + 1) * share, :],
            (((1, 2), (0, 2)), ((), ())),
            preferred_element_type=jnp.float32,
        ).astype(jnp.bfloat16)
        for h in range(halves)
    ]
    axis, bit, combined = bits[0]
    bit_axes = list(range(nbits - 1, -1, -1))
    ax = bit_axes.index(combined)
    mine = (lax.axis_index(axis) >> bit) & 1
    keeps = [lax.dynamic_index_in_dim(p, mine, ax, keepdims=False) for p in parts]
    sends = [lax.dynamic_index_in_dim(p, 1 - mine, ax, keepdims=False) for p in parts]
    received = [exchange(v, axis, bit) for v in sends]
    bit_axes.pop(ax)
    pieces = [keeps[s] + received[s] for s in range(3)]
    small_bits = index_bits(("rep",))
    axes_of = [list(bit_axes) for s in range(3)]
    for step in range(len(rest)):
        sends, keeps = [], []
        for s in range(3):
            axis, bit, combined = orders[s][step]
            ax = axes_of[s].index(combined)
            mine = (lax.axis_index(axis) >> bit) & 1
            keeps.append(lax.dynamic_index_in_dim(pieces[s], mine, ax, keepdims=False))
            sends.append(lax.dynamic_index_in_dim(pieces[s], 1 - mine, ax, keepdims=False))
            axes_of[s].pop(ax)
        received = []
        if step < len(small_bits):
            packed, sends[0] = lax.optimization_barrier((packed, sends[0]))
            received.append(exchange(packed, *small_bits[step]))
        received = [exchange(sends[s], orders[s][step][0], orders[s][step][1]) for s in range(3)] + received
        if step < halves:
            received, grad_chunks[step] = lax.optimization_barrier((received, grad_chunks[step]))
        else:
            received = lax.optimization_barrier(received)
        if step < len(small_bits):
            packed = packed + received.pop()
        pieces = [keeps[s] + received[s] for s in range(3)]
    grad_weight = jnp.concatenate(pieces, 1).reshape(rows, taps, out_chans)

    for step in range(len(rest), len(small_bits)):
        packed = packed + exchange(packed, *small_bits[step])
    grad_shift = packed[:out_chans] / mean_weight
    grad_gain = packed[out_chans : 2 * out_chans] / mean_weight
    grad_class = packed[2 * out_chans : (2 + classes) * out_chans].reshape(classes, out_chans) / mean_weight
    loss = packed[(2 + classes) * out_chans] / mean_weight / all_pix
    grad_features = jnp.concatenate(grad_chunks, 1).reshape(images, tile_rows, columns, in_chans)
    return (grad_features, grad_weight, grad_gain, grad_shift, grad_class, loss)


def solution(mesh):
    in_specs = (
        P("rep", "tile", None, None),
        P("rep", "tile", None, None),
        P(),
        P(),
        P(),
        P(),
        P("rep", "tile", None),
        P(),
    )
    out_specs = (P("rep", "tile", None, None), P(("rep", "tile"), None, None), P(), P(), P(), P())
    return jax.shard_map(body, mesh=mesh, in_specs=in_specs, out_specs=out_specs, check_vma=False)
```

```python
import jax
import jax.numpy as jnp
from jax import lax
from jax.sharding import PartitionSpec as P

IMG_DEV = 2
H = 48
W = 72
RATE = 12


def padded(x, sides, width):
    for axis, dim in sides:
        size, length = (lax.axis_size(axis), x.shape[dim])
        up = [(i, (i + 1) % size) for i in range(size - 1)]
        down = [(j, i) for i, j in up]
        last = lax.slice_in_dim(x, length - width, length, axis=dim)
        first = lax.slice_in_dim(x, 0, width, axis=dim)
        before = lax.ppermute(last, axis, up)
        after = lax.ppermute(first, axis, down)
        x = jnp.concatenate([before, x, after], axis=dim)
    return x


def index_bits(axes):
    bits = []
    for axis in reversed(axes):
        size = lax.axis_size(axis)
        assert size & (size - 1) == 0
        bits += [(axis, b) for b in range(size.bit_length() - 1)]
    return bits


def exchange(x, axis, bit):
    size = lax.axis_size(axis)
    pairs = [(i, i ^ (1 << bit)) for i in range(size)]
    return lax.ppermute(x, axis, pairs)


def butterfly_sum(x, axes):
    for axis, bit in index_bits(axes):
        x = jax.tree.map(lambda v, w: v + w, x, exchange(x, axis, bit))
    return x


def halving_scatter(x, steps, bit_axes):
    bit_axes = list(bit_axes)
    for axis, bit, combined in steps:
        ax = bit_axes.index(combined)
        mine = (lax.axis_index(axis) >> bit) & 1
        keep = lax.dynamic_index_in_dim(x, mine, ax, keepdims=False)
        send = lax.dynamic_index_in_dim(x, 1 - mine, ax, keepdims=False)
        x = keep + exchange(send, axis, bit)
        bit_axes.pop(ax)
    return x


def body(
    features,
    conv_out,
    conv_weight,
    norm_gain_vector,
    norm_shift_vector,
    class_map,
    labels,
    class_weight,
):
    highest = lax.Precision.HIGHEST
    images, tile_rows, columns, in_chans = features.shape
    out_chans = conv_out.shape[3]
    taps = conv_weight.shape[0]
    local_pix = images * tile_rows * columns
    per_replica_part = IMG_DEV * H * W
    all_pix = lax.axis_size("rep") * per_replica_part
    classes = class_map.shape[0]

    onehot = (
        labels.reshape(local_pix, 1) == jnp.arange(classes, dtype=jnp.int32)
    ).astype(jnp.float32)
    weights_pix = jnp.sum(onehot * class_weight.astype(jnp.float32), -1)

    yvals = conv_out.astype(jnp.float32).reshape(local_pix, out_chans)
    tiles = lax.axis_size("tile")
    local_sum = jnp.sum(yvals, 0)
    local_offset = yvals - local_sum / local_pix
    local_stats = jnp.concatenate(
        [local_sum, jnp.sum(local_offset * local_offset, 0), jnp.sum(weights_pix)[None]]
    )
    slot = (jnp.arange(tiles) == lax.axis_index("tile")).astype(jnp.float32)
    tile_stats = lax.psum(slot[:, None] * local_stats[None, :], "tile")
    tile_sums = tile_stats[:, :out_chans]
    column_sum = jnp.sum(tile_sums, 0)
    tile_means = tile_sums / local_pix - column_sum / per_replica_part
    variance = (
        jnp.sum(tile_stats[:, out_chans : 2 * out_chans] + local_pix * tile_means * tile_means, 0)
        / per_replica_part
    )
    weight_total = butterfly_sum(jnp.sum(tile_stats[:, 2 * out_chans]), ("rep",))
    centre_offset = yvals - column_sum / per_replica_part
    inverse_deviation = lax.rsqrt(variance + 1e-05)
    normalized_input = centre_offset * inverse_deviation
    preactivation_values = norm_gain_vector * normalized_input + norm_shift_vector
    zvals = jnp.maximum(preactivation_values, 0.0)
    logits = jnp.dot(zvals, class_map.T, precision=highest)
    top_val = jnp.max(logits, -1, keepdims=True)
    log_total = top_val[:, 0] + jnp.log(jnp.sum(jnp.exp(logits - top_val), -1))
    cross = log_total - jnp.sum(onehot * logits, -1)
    mean_weight = weight_total / all_pix
    probs = jnp.exp(logits - log_total[:, None])
    grad_logit = weights_pix[:, None] * (probs - onehot)
    class_local_slice = jnp.dot(grad_logit.T, zvals, precision=highest)
    grad_z = jnp.dot(grad_logit, class_map, precision=highest)
    preactivation_gradient = jnp.where(preactivation_values > 0, grad_z, 0.0)
    first_gradient_sum, second_gradient_sum, class_tile, loss_tile = lax.psum(
        (
            jnp.sum(preactivation_gradient, 0),
            jnp.sum(preactivation_gradient * normalized_input, 0),
            class_local_slice,
            jnp.sum(weights_pix * cross),
        ),
        "tile",
    )
    packed = jnp.concatenate(
        [first_gradient_sum, second_gradient_sum, class_tile.reshape(-1), loss_tile[None]]
    )
    normalized_output_gradient = (
        norm_gain_vector
        * inverse_deviation
        * (
            (
                preactivation_gradient
                - first_gradient_sum / per_replica_part
                - normalized_input * second_gradient_sum / per_replica_part
            )
            / mean_weight
        )
    ).astype(jnp.bfloat16)
    normalized_output_gradient = normalized_output_gradient.reshape(
        images, tile_rows, columns, out_chans
    )
    column_pad = ((0, 0), (0, 0), (RATE, RATE), (0, 0))
    extended = jnp.pad(padded(normalized_output_gradient, (("tile", 1),), RATE), column_pad)
    own_rows = jnp.pad(normalized_output_gradient, column_pad)
    shifted_list = []
    for tap_index in range(taps):
        row_off = RATE - (tap_index // 3 - 1) * RATE
        col_off = RATE - (tap_index % 3 - 1) * RATE
        if tap_index // 3 == 1:
            piece = own_rows[:, :, col_off : col_off + columns, :]
        else:
            piece = extended[:, row_off : row_off + tile_rows, col_off : col_off + columns, :]
        shifted_list.append(piece.reshape(local_pix, out_chans))
    shifted = jnp.concatenate(shifted_list, 1)

    blocks = lax.axis_size("rep") * lax.axis_size("tile")
    nbits = blocks.bit_length() - 1
    rows = in_chans // blocks
    flat_x = features.reshape(local_pix, in_chans)
    packed, flat_x = lax.optimization_barrier((packed, flat_x))
    bits = [(axis, bit, combined) for combined, (axis, bit) in enumerate(index_bits(("rep", "tile")))]
    rest = bits[1:]
    orders = [rest, rest[1:] + rest[:1], rest[2:3] + rest[:2] + rest[3:]]
    group_taps = [taps - 2 * (taps // 3), taps // 3, taps // 3]
    starts = [sum(group_taps[:s]) for s in range(3)]
    parts = []
    for s in range(3):
        cols = jnp.concatenate(shifted_list[starts[s] : starts[s] + group_taps[s]], 1)
        part = lax.dot_general(
            flat_x, cols, (((0,), (0,)), ((), ())), preferred_element_type=jnp.float32
        )
        parts.append(part.reshape((2,) * nbits + (rows, group_taps[s] * out_chans)))

    halves = 2
    share = in_chans // halves
    grad_chunks = [
        lax.dot_general(
            shifted.reshape(local_pix, taps, out_chans),
            conv_weight[:, h * share : (h + 1) * share, :],
            (((1, 2), (0, 2)), ((), ())),
            preferred_element_type=jnp.float32,
        ).astype(jnp.bfloat16)
        for h in range(halves)
    ]
    axis, bit, combined = bits[0]
    bit_axes = list(range(nbits - 1, -1, -1))
    ax = bit_axes.index(combined)
    mine = (lax.axis_index(axis) >> bit) & 1
    keeps = [lax.dynamic_index_in_dim(p, mine, ax, keepdims=False) for p in parts]
    sends = [lax.dynamic_index_in_dim(p, 1 - mine, ax, keepdims=False) for p in parts]
    received = lax.optimization_barrier([exchange(v, axis, bit) for v in sends])
    bit_axes.pop(ax)
    pieces = [keeps[s] + received[s] for s in range(3)]
    small_bits = index_bits(("rep",))
    axes_of = [list(bit_axes) for s in range(3)]
    for step in range(len(rest)):
        sends, keeps = [], []
        for s in range(3):
            axis, bit, combined = orders[s][step]
            ax = axes_of[s].index(combined)
            mine = (lax.axis_index(axis) >> bit) & 1
            keeps.append(lax.dynamic_index_in_dim(pieces[s], mine, ax, keepdims=False))
            sends.append(lax.dynamic_index_in_dim(pieces[s], 1 - mine, ax, keepdims=False))
            axes_of[s].pop(ax)
        received = []
        small = step - 1
        if 0 <= small < len(small_bits):
            packed, sends = lax.optimization_barrier((packed, sends))
            received.append(exchange(packed, *small_bits[small]))
        received = [exchange(sends[s], orders[s][step][0], orders[s][step][1]) for s in range(3)] + received
        if step < halves:
            received, grad_chunks[step] = lax.optimization_barrier((received, grad_chunks[step]))
        else:
            received = lax.optimization_barrier(received)
        if 0 <= small < len(small_bits):
            packed = packed + received.pop()
        pieces = [keeps[s] + received[s] for s in range(3)]
    grad_weight = jnp.concatenate(pieces, 1).reshape(rows, taps, out_chans)

    for small in range(len(rest) - 1, len(small_bits)):
        packed = packed + exchange(packed, *small_bits[small])
    grad_shift = packed[:out_chans] / mean_weight
    grad_gain = packed[out_chans : 2 * out_chans] / mean_weight
    grad_class = packed[2 * out_chans : (2 + classes) * out_chans].reshape(classes, out_chans) / mean_weight
    loss = packed[(2 + classes) * out_chans] / mean_weight / all_pix
    grad_features = jnp.concatenate(grad_chunks, 1).reshape(images, tile_rows, columns, in_chans)
    return (grad_features, grad_weight, grad_gain, grad_shift, grad_class, loss)


def solution(mesh):
    in_specs = (
        P("rep", "tile", None, None),
        P("rep", "tile", None, None),
        P(),
        P(),
        P(),
        P(),
        P("rep", "tile", None),
        P(),
    )
    out_specs = (P("rep", "tile", None, None), P(("rep", "tile"), None, None), P(), P(), P(), P())
    return jax.shard_map(body, mesh=mesh, in_specs=in_specs, out_specs=out_specs, check_vma=False)
```
